128 devices in a mesh: gx: 16 (over y_hi, x, core), gy: 8 (over z, y_lo).
Axes of the slice: x: 4, y: 4 (y_hi: 2, y_lo: 2; y = y_hi * 2 + y_lo), z: 4, core: 2. Of those that a mesh axis runs over, the one named last changes fastest.
Arguments:
- fv_state: float32 [4, 128, 128, 1024], P(None, 'gx', 'gy'), may hold values from -6 to 6
- buffer_owner: int32 [131072, 1], P(('gx', 'gy')), may hold values from 0 to 127; in each aligned block of 1024 rows (0 to 1023, 1024 to 2047, ...) at most 16 rows name the same one
- buffer_cell: int32 [131072], P(('gx', 'gy')), may hold values from 0 to 131071
- buffer_frac: float32 [3, 131072], P(None, ('gx', 'gy')), may hold values from 0 to 1
- buffer_count: int32 [128], P(('gx', 'gy')), may hold values from 341 to 1024, as said below
- sph_offset: float32 [3, 64, 32, 128], P(None, 'gx', 'gy'), may hold values from 0 to 1
- sph_vel: float32 [3, 64, 32, 128], P(None, 'gx', 'gy'), may hold values from -6 to 6
- sph_press: float32 [64, 32, 128], P('gx', 'gy'), may hold values from 0.1 to 1
- tile_count: int32 [64, 32], P('gx', 'gy'), may hold values from 64 to 128
Outputs:
- fv_next: float32 [4, 128, 128, 1024], P(None, 'gx', 'gy')
- buffer_state: float32 [4, 131072], P(None, ('gx', 'gy'))
- sph_accel: float32 [3, 64, 32, 128], P(None, 'gx', 'gy')
The draws below stay inside these ranges and needn't reach their ends.
Inputs may be any that keep to these rules, and one draw needn't show every extreme that they name: `buffer_owner`: among the 1024 rows of one device, no owner is named by more than 16 rows, a bound that some block reaches. `buffer_count`: the live buffer slots of a device are its first ones; some device has 1024 live slots and some has 341. `tile_count`: the live particles of a tile occupy its first slots.
All inputs are finite; a program needn't handle non-finite values.
Results may differ from the reference program's by a relative error of at most 0.0003.
Values sent between devices are 32-bit elements; how exact they have to be, the bound alone decides.
No kernel may reach another device: no remote copies, remote signals or barrier semaphores. Data moves between devices by JAX's collectives and lax.ppermute only.
A program may use at most 256 MiB of HBM per device.

```python
import math
import jax
import jax.numpy as jnp
import numpy as np
from jax import lax

CX = 8
CY = 16
CZ = 1024
BUF_DEV = 1024
PT = 128
NX = 128
NY = 128
NBUF = 131072
CAP = 16
NTX = 64
NTY = 32
N_GX = 16
N_GY = 8
DEVICES = 128


def draw_buffer_count(key, part):
    first_key, second_key = jax.random.split(jax.random.fold_in(key, 11))
    counts = jax.random.randint(first_key, (DEVICES,), BUF_DEV // 3, BUF_DEV + 1)
    order = jax.random.permutation(second_key, DEVICES)
    counts = counts.at[order[0]].set(BUF_DEV).at[order[1]].set(BUF_DEV // 3)
    return counts.astype(jnp.int32)


def with_ends(values, own_key, least, largest):
    extent = values.shape
    place = [jax.random.randint(jax.random.fold_in(own_key, axis), (), 0, extent[axis]) for axis in range(len(extent))]
    values = values.at[tuple(place)].set(least)
    longest = extent.index(max(extent))
    place[longest] = (place[longest] + 1) % extent[longest]
    return values.at[tuple(place)].set(largest)


def shard_levels(key, extent, cuts, low, high):
    def one(dim, parts):
        steps = jax.random.uniform(jax.random.fold_in(jax.random.fold_in(key, 6), dim), (parts,), jnp.float32, low / len(cuts), high / len(cuts))
        return jnp.repeat(jnp.exp(steps), extent[dim] // parts).reshape((-1,) + (1,) * (len(extent) - dim - 1))

    factor_of = one(*cuts[0])
    for cut in cuts[1:]:
        factor_of = factor_of * one(*cut)
    return factor_of


def routed_block(own_key, own, number, rows, amount, top, bound, lean):
    order = jax.random.permutation(own_key, amount)
    crowded, ordinary = shares(amount, rows * top, bound, lean, True), shares(amount, rows * top, bound, lean, False)
    places = jnp.arange(amount)

    def named(tallies, turn):
        used = int((tallies > 0).sum())
        fixed = max(1, used // 4)
        passed = fixed + (places - fixed + turn * (used - fixed)) % max(1, amount - fixed)
        return jnp.zeros((amount,), jnp.int32).at[order[jnp.where(places < fixed, places, passed)]].set(jnp.asarray(tallies, jnp.int32))

    tallies = jnp.where(number % 4 == 0, named(crowded, number // 4), named(ordinary, number - number // 4 - 1))
    mixed = jax.random.permutation(jax.random.fold_in(own, 3), amount)
    source_of, taker = mixed[0:amount // 2 * 2:2], mixed[1:amount // 2 * 2:2]
    margin = jnp.minimum(tallies[source_of] - 1, bound - tallies[taker]) // 2
    margin = jnp.where((source_of == order[0]) | (taker == order[0]) | (tallies[taker] == 0), 0, jnp.maximum(margin, 0))
    passed = jax.random.randint(jax.random.fold_in(own, 4), (amount // 2,), 0, 1 << 20) % (margin + 1)
    tallies = tallies.at[source_of].add(-passed).at[taker].add(passed)
    members = jnp.searchsorted(jnp.cumsum(tallies), jnp.arange(rows * top), side="right").astype(jnp.int32)
    table = members.reshape(top, rows).T
    table = table[jax.random.permutation(jax.random.fold_in(own, 1), rows)]
    turn = jax.random.randint(jax.random.fold_in(own, 2), (rows, 1), 0, top)
    return jnp.take_along_axis(table, (jnp.arange(top)[None, :] + turn) % top, axis=1)


def shares(count, total, most, lean, full):
    weights = [(1 << 20) // math.isqrt(grade ** lean) + 1 for grade in range(1, count + 1)]
    largest = most if full else min(most, max(-(-total // count), total * weights[0] // sum(weights)))
    least = 1 if total - largest >= count - 1 else 0
    holding, rest = [largest] + [least] * (count - 1), total - largest - least * (count - 1)
    while rest > 0:
        movable = [i for i in range(1, count) if holding[i] < largest] or [i for i in range(1, count) if holding[i] < most]
        mass, remaining = sum([weights[i] for i in movable]), rest
        for i in movable:
            extra = min(most - holding[i], max(1, remaining * weights[i] // mass), rest)
            holding[i] = holding[i] + extra
            rest = rest - extra
    return np.array(holding)


def scatter_about(stream_key, extent, spread, most, cuts=(), kind=jnp.bfloat16):
    loudness = shard_levels(stream_key, extent, cuts, -0.22, 0.18) if cuts else 1.0
    entries = jax.random.normal(stream_key, extent, jnp.float32) * spread * loudness
    return jnp.minimum(jnp.maximum(entries, -most), most).astype(kind)


def setup_inputs(seed: int = 0) -> dict:
    streams_of = jax.random.split(jax.random.key(seed), 10)
    fv_state = scatter_about(streams_of[0], (4, NX, NY, CZ), 1.0, 6.0, ((1, 16), (2, 8)), jnp.float32)
    buffer_owner_keys = jax.random.split(jax.random.fold_in(streams_of[1], 1), NBUF // BUF_DEV)
    buffer_owner_turns = jax.random.permutation(jax.random.fold_in(streams_of[1], 3), NBUF // BUF_DEV)
    buffer_owner = jax.vmap(lambda own, number: routed_block(jax.random.fold_in(streams_of[1], 2), own, number, BUF_DEV, DEVICES, 1, CAP, 2))(buffer_owner_keys, buffer_owner_turns).reshape((NBUF, 1))
    buffer_cell = with_ends(jax.random.randint(streams_of[2], (NBUF,), 0, CX * CY * CZ), jax.random.fold_in(streams_of[2], 1), 0, (CX * CY * CZ) - 1).astype(jnp.int32)
    buffer_frac = jnp.clip(1.0 * jax.random.uniform(streams_of[3], (3, NBUF), jnp.float32) ** shard_levels(streams_of[3], (3, NBUF), ((1, 128),), -0.2, 0.2), 0.0, 1.0)
    buffer_count = draw_buffer_count(jax.random.fold_in(streams_of[9], 71), 0)
    sph_offset = jnp.clip(1.0 * jax.random.uniform(streams_of[5], (3, NTX, NTY, PT), jnp.float32) ** shard_levels(streams_of[5], (3, NTX, NTY, PT), ((1, 16), (2, 8)), -0.2, 0.2), 0.0, 1.0)
    sph_vel = scatter_about(streams_of[6], (3, NTX, NTY, PT), 1.0, 6.0, ((1, 16), (2, 8)), jnp.float32)
    sph_press = jnp.clip(jnp.exp(math.log(1.0) - 2.3025851 * jax.random.uniform(streams_of[7], (NTX, NTY, PT), jnp.float32) ** shard_levels(streams_of[7], (NTX, NTY, PT), ((0, 16), (1, 8)), -0.2, 0.2)), 0.1, 1.0)
    tile_count = with_ends(jax.random.randint(streams_of[8], (NTX, NTY), 64, PT + 1), jax.random.fold_in(streams_of[8], 1), 64, PT).astype(jnp.int32)
    return dict(fv_state=fv_state, buffer_owner=buffer_owner, buffer_cell=buffer_cell, buffer_frac=buffer_frac, buffer_count=buffer_count, sph_offset=sph_offset, sph_vel=sph_vel, sph_press=sph_press, tile_count=tile_count)


STEP_RATIO = 0.3
VISCOSITY = 0.02
FORCE_SCALE = 0.1

def face_flux(left_side, right_side, normal):
    jump_term = right_side - left_side
    fluxes = [-0.5 * jump_term[channel] for channel in range(4)]
    fluxes[0] = fluxes[0] + 0.5 * (left_side[normal] + right_side[normal])
    fluxes[normal] = fluxes[normal] + 0.5 * (left_side[0] + right_side[0])
    return jnp.stack(fluxes)

def flux_step(padded):
    interior = padded[:, 1:-1, 1:-1, 1:-1]
    slab_rows = padded[:, :, 1:-1, 1:-1]
    across = face_flux(slab_rows[:, :-1], slab_rows[:, 1:], 1)
    change = across[:, 1:] - across[:, :-1]
    slab_rows = padded[:, 1:-1, :, 1:-1]
    across = face_flux(slab_rows[:, :, :-1], slab_rows[:, :, 1:], 2)
    change = change + (across[:, :, 1:] - across[:, :, :-1])
    slab_rows = padded[:, 1:-1, 1:-1, :]
    across = face_flux(slab_rows[:, :, :, :-1], slab_rows[:, :, :, 1:], 3)
    change = change + (across[:, :, :, 1:] - across[:, :, :, :-1])
    return interior - STEP_RATIO * change

def trilinear(upper, fractions, base_x, base_y, base_z):
    extent_y = upper.shape[2]
    extent_z = upper.shape[3]
    flat_field = upper.reshape(upper.shape[0], -1)
    values = jnp.zeros((upper.shape[0], base_x.shape[0]), jnp.float32)
    for corner in range(8):
        step_x = corner // 4
        step_y = corner // 2 % 2
        step_z = corner % 2
        factor_x = fractions[0] if step_x else 1.0 - fractions[0]
        factor_y = fractions[1] if step_y else 1.0 - fractions[1]
        factor_z = fractions[2] if step_z else 1.0 - fractions[2]
        position = ((base_x + step_x) * extent_y + base_y + step_y) * extent_z + base_z + step_z
        values = values + factor_x * factor_y * factor_z * jnp.take(flat_field, position, axis=1)
    return values

def pair_accel(own_tiles, other_tiles, shift_x, shift_y):
    separation_x = own_tiles[0][:, :, None] - other_tiles[0][:, None, :] - shift_x
    separation_y = own_tiles[1][:, :, None] - other_tiles[1][:, None, :] - shift_y
    separation_z = own_tiles[2][:, :, None] - other_tiles[2][:, None, :]
    distance = jnp.sqrt(separation_x * separation_x + separation_y * separation_y + separation_z * separation_z)
    closeness = jnp.maximum(1.0 - distance, 0.0)
    weight = 20.0 * closeness * closeness * closeness * other_tiles[7][:, None, :]
    push_term = (own_tiles[6][:, :, None] + other_tiles[6][:, None, :]) * weight
    weight_total = lax.optimization_barrier(jnp.sum(weight, axis=-1))
    result = []
    for channel, separation in enumerate((separation_x, separation_y, separation_z)):
        drag_term = lax.optimization_barrier(jnp.sum(weight * other_tiles[3 + channel][:, None, :], axis=-1)) - weight_total * own_tiles[3 + channel]
        result.append(lax.optimization_barrier(jnp.sum(push_term * separation, axis=-1)) + VISCOSITY * drag_term)
    return jnp.stack(result)

def reference(fv_state, buffer_owner, buffer_cell, buffer_frac, buffer_count, sph_offset, sph_vel, sph_press, tile_count):
    padded = jnp.pad(fv_state, ((0, 0), (1, 1), (1, 1), (1, 1)))

    def block_step(block_index):
        piece = lax.dynamic_slice_in_dim(padded, block_index * CX, CX + 2, 1)
        return flux_step(piece)
    blocks = lax.map(block_step, jnp.arange(N_GX, dtype=jnp.int32))
    fv_next = jnp.transpose(blocks, (1, 0, 2, 3, 4)).reshape(4, NX, NY, CZ)
    upper = jnp.pad(fv_next, ((0, 0), (0, 1), (0, 1), (0, 1)))
    owner_ids = buffer_owner[:, 0]
    cell_x = buffer_cell // (CY * CZ)
    cell_y = buffer_cell // CZ % CY
    cell_z = buffer_cell % CZ
    base_x = owner_ids // N_GY * CX + cell_x
    base_y = owner_ids % N_GY * CY + cell_y
    values = trilinear(upper, buffer_frac, base_x, base_y, cell_z)
    slot_ids = jnp.arange(NBUF, dtype=jnp.int32)
    is_live = slot_ids % BUF_DEV < buffer_count[slot_ids // BUF_DEV]
    buffer_state = jnp.where(is_live[None, :], values, 0.0)
    particle_slots = jnp.arange(PT, dtype=jnp.int32)
    tile_live = (particle_slots[None, None, :] < tile_count[:, :, None]).astype(jnp.float32)
    packed = jnp.concatenate([sph_offset, sph_vel, sph_press[None], tile_live[None]], axis=0)
    framed = jnp.pad(packed, ((0, 0), (1, 1), (1, 1), (0, 0)))

    def tile_row(row_index):
        own_tiles = lax.dynamic_index_in_dim(packed, row_index, 1, keepdims=False)
        total = jnp.zeros((3, NTY, PT), jnp.float32)
        for corner in range(9):
            step_x = corner // 3 - 1
            step_y = corner % 3 - 1
            other_row = lax.dynamic_index_in_dim(framed, row_index + 1 + step_x, 1, keepdims=False)
            other_tiles = other_row[:, 1 + step_y:1 + step_y + NTY]
            total = total + pair_accel(own_tiles, other_tiles, float(step_x), float(step_y))
        return FORCE_SCALE * total * own_tiles[7][None]
    accel_rows = lax.map(tile_row, jnp.arange(NTX, dtype=jnp.int32))
    sph_accel = jnp.transpose(accel_rows, (1, 0, 2, 3))
    return (fv_next, buffer_state, sph_accel)
```

```python
import jax
import jax.numpy as jnp
from jax import lax
from jax.sharding import PartitionSpec as P

STEP_RATIO = 0.3
VISCOSITY = 0.02
FORCE_SCALE = 0.1


def padded_2(array, sides, width):
    for axis, dim in sides:
        count, length = (lax.axis_size(axis), array.shape[dim])
        up = [(i, (i + 1) % count) for i in range(count - 1)]
        down = [(j, i) for i, j in up]
        last = lax.slice_in_dim(array, length - width, length, axis=dim)
        leading = lax.slice_in_dim(array, 0, width, axis=dim)
        before = lax.ppermute(last, axis, up)
        after = lax.ppermute(leading, axis, down)
        array = jnp.concatenate([before, array, after], axis=dim)
    return array


def from_behind(array, axis, by):
    count = lax.axis_size(axis)
    pairs = [(i, i + by) for i in range(count) if 0 <= i + by < count]
    return lax.ppermute(array, axis, pairs)


def face_flux(left_side, right_side, normal):
    jump_term = right_side - left_side
    fluxes = [-0.5 * jump_term[channel] for channel in range(4)]
    fluxes[0] = fluxes[0] + 0.5 * (left_side[normal] + right_side[normal])
    fluxes[normal] = fluxes[normal] + 0.5 * (left_side[0] + right_side[0])
    return jnp.stack(fluxes)


def flux_step(padded):
    interior = padded[:, 1:-1, 1:-1, 1:-1]
    slab_rows = padded[:, :, 1:-1, 1:-1]
    across = face_flux(slab_rows[:, :-1], slab_rows[:, 1:], 1)
    change = across[:, 1:] - across[:, :-1]
    slab_rows = padded[:, 1:-1, :, 1:-1]
    across = face_flux(slab_rows[:, :, :-1], slab_rows[:, :, 1:], 2)
    change = change + (across[:, :, 1:] - across[:, :, :-1])
    slab_rows = padded[:, 1:-1, 1:-1, :]
    across = face_flux(slab_rows[:, :, :, :-1], slab_rows[:, :, :, 1:], 3)
    change = change + (across[:, :, :, 1:] - across[:, :, :, :-1])
    return interior - STEP_RATIO * change


def answer_requests(upper, arrived):
    channels, extent_x, extent_y, cells_z = upper.shape
    cells_y = extent_y - 1
    count = arrived.shape[1]
    cell_index = arrived[3].astype(jnp.int32)
    base_x = cell_index // (cells_y * cells_z)
    base_y = cell_index // cells_z % cells_y
    base_z = cell_index % cells_z
    frac_x, frac_y, frac_z = arrived[0], arrived[1], arrived[2]
    z_ids = lax.broadcasted_iota(jnp.int32, (cells_z, count), 0)
    z_weight = jnp.where(z_ids == base_z[None, :], 1.0 - frac_z[None, :], 0.0) + jnp.where(
        z_ids == base_z[None, :] + 1, frac_z[None, :], 0.0
    )
    columns = lax.dot_general(
        upper,
        z_weight,
        (((3,), (0,)), ((), ())),
        precision=lax.Precision.HIGH,
        preferred_element_type=jnp.float32,
    )
    x_ids = lax.broadcasted_iota(jnp.int32, (extent_x, 1, count), 0)
    y_ids = lax.broadcasted_iota(jnp.int32, (1, extent_y, count), 1)
    weight_x = jnp.where(x_ids == base_x, 1.0 - frac_x, 0.0) + jnp.where(x_ids == base_x + 1, frac_x, 0.0)
    weight_y = jnp.where(y_ids == base_y, 1.0 - frac_y, 0.0) + jnp.where(y_ids == base_y + 1, frac_y, 0.0)
    return jnp.sum(columns * (weight_x * weight_y)[None], axis=(1, 2))


def pair_accel(own_tiles, other_tiles, shift_x, shift_y):
    separation_x = own_tiles[0][:, :, None] - other_tiles[0][:, None, :] - shift_x
    separation_y = own_tiles[1][:, :, None] - other_tiles[1][:, None, :] - shift_y
    separation_z = own_tiles[2][:, :, None] - other_tiles[2][:, None, :]
    distance = jnp.sqrt(
        separation_x * separation_x + separation_y * separation_y + separation_z * separation_z
    )
    closeness = jnp.maximum(1.0 - distance, 0.0)
    weight = 20.0 * closeness * closeness * closeness * other_tiles[7][:, None, :]
    push_term = (own_tiles[6][:, :, None] + other_tiles[6][:, None, :]) * weight
    weight_total = jnp.sum(weight, axis=-1)
    result = []
    for channel, separation in enumerate((separation_x, separation_y, separation_z)):
        drag_term = (
            jnp.sum(weight * other_tiles[3 + channel][:, None, :], axis=-1)
            - weight_total * own_tiles[3 + channel]
        )
        result.append(jnp.sum(push_term * separation, axis=-1) + VISCOSITY * drag_term)
    return jnp.stack(result)


def per_device(
    fv_state,
    buffer_owner,
    buffer_cell,
    buffer_frac,
    buffer_count,
    sph_offset,
    sph_vel,
    sph_press,
    tile_count,
):
    grid_x = lax.axis_size("gx")
    grid_y = lax.axis_size("gy")
    z_margin = ((0, 0), (0, 0), (0, 0), (1, 1))
    bordered = padded_2(fv_state, (("gx", 1), ("gy", 2)), 1)
    fv_next = flux_step(jnp.pad(bordered, z_margin))
    next_rows = from_behind(fv_next[:, :1], "gx", -1)
    widened_rows = jnp.concatenate([fv_next, next_rows], axis=1)
    next_columns = from_behind(widened_rows[:, :, :1], "gy", -1)
    upper = jnp.concatenate([widened_rows, next_columns], axis=2)
    devices = grid_x * grid_y
    buffer_rows = buffer_cell.shape[0]
    capacity = 2 * buffer_rows // devices
    slot_total = devices * capacity
    owner_ids = buffer_owner[:, 0]
    row_ids = jnp.arange(buffer_rows, dtype=jnp.int32)
    is_live = row_ids < buffer_count[0]
    one_hot = (owner_ids[:, None] == jnp.arange(devices, dtype=jnp.int32)[None, :]) & is_live[
        :, None
    ]
    one_hot_float = one_hot.astype(jnp.bfloat16)
    lower_mask = (row_ids[None, :] < row_ids[:, None]).astype(jnp.bfloat16)
    earlier = jnp.dot(lower_mask, one_hot_float, preferred_element_type=jnp.float32)
    ranks = jnp.sum(jnp.where(one_hot, earlier, 0.0), axis=1).astype(jnp.int32)
    target = jnp.where(is_live, owner_ids * capacity + ranks, slot_total)
    selector = (target[:, None] == jnp.arange(slot_total, dtype=jnp.int32)[None, :]).astype(
        jnp.float32
    )
    request = jnp.concatenate([buffer_frac, buffer_cell[None].astype(jnp.float32)], axis=0)
    outgoing = jnp.dot(
        request, selector, precision=lax.Precision.HIGHEST, preferred_element_type=jnp.float32
    )
    arrived = lax.all_to_all(outgoing, ("gx", "gy"), split_axis=1, concat_axis=1, tiled=True)
    returned = lax.all_to_all(
        answer_requests(upper, arrived), ("gx", "gy"), split_axis=1, concat_axis=1, tiled=True
    )
    picked = lax.dot_general(
        returned,
        selector,
        (((1,), (1,)), ((), ())),
        precision=lax.Precision.HIGHEST,
        preferred_element_type=jnp.float32,
    )
    buffer_state = jnp.where(is_live[None, :], picked, 0.0)
    tiles_x, tiles_y, tile_slots = sph_press.shape
    tile_live = (
        jnp.arange(tile_slots, dtype=jnp.int32)[None, None, :] < tile_count[:, :, None]
    ).astype(jnp.float32)
    packed = jnp.concatenate([sph_offset, sph_vel, sph_press[None], tile_live[None]], axis=0)
    framed = padded_2(packed, (("gx", 1), ("gy", 2)), 1)
    own_tiles = packed.reshape(8, tiles_x * tiles_y, tile_slots)
    total = jnp.zeros((3, tiles_x * tiles_y, tile_slots), jnp.float32)
    for corner in range(9):
        step_x = corner // 3 - 1
        step_y = corner % 3 - 1
        other_tiles = framed[
            :, 1 + step_x : 1 + step_x + tiles_x, 1 + step_y : 1 + step_y + tiles_y
        ].reshape(8, tiles_x * tiles_y, tile_slots)
        total = total + pair_accel(own_tiles, other_tiles, float(step_x), float(step_y))
    sph_accel = (FORCE_SCALE * total * own_tiles[7][None]).reshape(3, tiles_x, tiles_y, tile_slots)
    return (fv_next, buffer_state, sph_accel)


def solution(mesh):
    return jax.shard_map(
        per_device,
        mesh=mesh,
        in_specs=(
            P(None, "gx", "gy", None),
            P(("gx", "gy"), None),
            P(("gx", "gy")),
            P(None, ("gx", "gy")),
            P(("gx", "gy")),
            P(None, "gx", "gy", None),
            P(None, "gx", "gy", None),
            P("gx", "gy", None),
            P("gx", "gy"),
        ),
        out_specs=(P(None, "gx", "gy", None), P(None, ("gx", "gy")), P(None, "gx", "gy", None)),
        check_vma=False,
    )
```

```python
import jax
import jax.numpy as jnp
from jax import lax
from jax.sharding import PartitionSpec as P

STEP_RATIO = 0.3
VISCOSITY = 0.02
FORCE_SCALE = 0.1


def padded_2(array, sides, width):
    for axis, dim in sides:
        count, length = (lax.axis_size(axis), array.shape[dim])
        up = [(i, (i + 1) % count) for i in range(count - 1)]
        down = [(j, i) for i, j in up]
        last = lax.slice_in_dim(array, length - width, length, axis=dim)
        leading = lax.slice_in_dim(array, 0, width, axis=dim)
        before = lax.ppermute(last, axis, up)
        after = lax.ppermute(leading, axis, down)
        array = jnp.concatenate([before, array, after], axis=dim)
    return array


def from_behind(array, axis, by):
    count = lax.axis_size(axis)
    pairs = [(i, i + by) for i in range(count) if 0 <= i + by < count]
    return lax.ppermute(array, axis, pairs)


def face_flux(left_side, right_side, normal):
    jump_term = right_side - left_side
    fluxes = [-0.5 * jump_term[channel] for channel in range(4)]
    fluxes[0] = fluxes[0] + 0.5 * (left_side[normal] + right_side[normal])
    fluxes[normal] = fluxes[normal] + 0.5 * (left_side[0] + right_side[0])
    return jnp.stack(fluxes)


def flux_sweep(state, x_lo, x_hi, y_lo, y_hi):
    slab = jnp.concatenate([x_lo, state, x_hi], axis=1)
    across = face_flux(slab[:, :-1], slab[:, 1:], 1)
    change = across[:, 1:] - across[:, :-1]
    slab = jnp.concatenate([y_lo, state, y_hi], axis=2)
    across = face_flux(slab[:, :, :-1], slab[:, :, 1:], 2)
    change = change + (across[:, :, 1:] - across[:, :, :-1])
    slab = jnp.pad(state, ((0, 0), (0, 0), (0, 0), (1, 1)))
    across = face_flux(slab[:, :, :, :-1], slab[:, :, :, 1:], 3)
    change = change + (across[:, :, :, 1:] - across[:, :, :, :-1])
    return state - STEP_RATIO * change


def from_diagonal(array):
    count_x = lax.axis_size("gx")
    count_y = lax.axis_size("gy")
    pairs = [
        ((i + 1) * count_y + j + 1, i * count_y + j)
        for i in range(count_x - 1)
        for j in range(count_y - 1)
    ]
    return lax.ppermute(array, ("gx", "gy"), pairs)


def answer_requests(main, extra, arrived):
    channels, cells_x, cells_y, cells_z = main.shape
    count = arrived.shape[1]
    cell_index = arrived[3].astype(jnp.int32)
    base_x = cell_index // (cells_y * cells_z)
    base_y = cell_index // cells_z % cells_y
    base_z = cell_index % cells_z
    frac_x, frac_y, frac_z = arrived[0], arrived[1], arrived[2]
    z_ids = lax.broadcasted_iota(jnp.int32, (cells_z, count), 0)
    z_weight = jnp.where(z_ids == base_z[None, :], 1.0 - frac_z[None, :], 0.0) + jnp.where(
        z_ids == base_z[None, :] + 1, frac_z[None, :], 0.0
    )

    def contract(part):
        return lax.dot_general(
            part,
            z_weight,
            (((part.ndim - 1,), (0,)), ((), ())),
            precision=lax.Precision.HIGH,
            preferred_element_type=jnp.float32,
        )

    x_ids = lax.broadcasted_iota(jnp.int32, (cells_x, count), 0)
    y_ids = lax.broadcasted_iota(jnp.int32, (cells_y, count), 0)
    weight_x = jnp.where(x_ids == base_x, 1.0 - frac_x, 0.0) + jnp.where(x_ids == base_x + 1, frac_x, 0.0)
    weight_y = jnp.where(y_ids == base_y, 1.0 - frac_y, 0.0) + jnp.where(y_ids == base_y + 1, frac_y, 0.0)
    edge_x = jnp.where(base_x + 1 == cells_x, frac_x, 0.0)
    edge_y = jnp.where(base_y + 1 == cells_y, frac_y, 0.0)
    weight_main = weight_x[:, None, :] * weight_y[None, :, :]
    weight_extra = jnp.concatenate(
        [edge_x[None] * weight_y, weight_x * edge_y[None], (edge_x * edge_y)[None]], axis=0
    )
    values = jnp.sum(contract(main) * weight_main[None], axis=(1, 2))
    return values + jnp.sum(contract(extra) * weight_extra[None], axis=1)


def pair_accel(own_tiles, other_tiles, shift_x, shift_y):
    separation_x = own_tiles[0][:, :, None] - other_tiles[0][:, None, :] - shift_x
    separation_y = own_tiles[1][:, :, None] - other_tiles[1][:, None, :] - shift_y
    separation_z = own_tiles[2][:, :, None] - other_tiles[2][:, None, :]
    distance = jnp.sqrt(
        separation_x * separation_x + separation_y * separation_y + separation_z * separation_z
    )
    closeness = jnp.maximum(1.0 - distance, 0.0)
    weight = 20.0 * closeness * closeness * closeness * other_tiles[7][:, None, :]
    push_term = (own_tiles[6][:, :, None] + other_tiles[6][:, None, :]) * weight
    weight_total = jnp.sum(weight, axis=-1)
    result = []
    for channel, separation in enumerate((separation_x, separation_y, separation_z)):
        drag_term = (
            jnp.sum(weight * other_tiles[3 + channel][:, None, :], axis=-1)
            - weight_total * own_tiles[3 + channel]
        )
        result.append(jnp.sum(push_term * separation, axis=-1) + VISCOSITY * drag_term)
    return jnp.stack(result)


def per_device(
    fv_state,
    buffer_owner,
    buffer_cell,
    buffer_frac,
    buffer_count,
    sph_offset,
    sph_vel,
    sph_press,
    tile_count,
):
    grid_x = lax.axis_size("gx")
    grid_y = lax.axis_size("gy")
    x_lo = from_behind(fv_state[:, -1:], "gx", 1)
    x_hi = from_behind(fv_state[:, :1], "gx", -1)
    y_lo = from_behind(fv_state[:, :, -1:], "gy", 1)
    y_hi = from_behind(fv_state[:, :, :1], "gy", -1)
    fv_next = flux_sweep(fv_state, x_lo, x_hi, y_lo, y_hi)
    row_next = from_behind(fv_next[:, 0], "gx", -1)
    column_next = from_behind(fv_next[:, :, 0], "gy", -1)
    corner_next = from_diagonal(fv_next[:, 0, 0])
    extra = jnp.concatenate([row_next, column_next, corner_next[:, None]], axis=1)
    devices = grid_x * grid_y
    buffer_rows = buffer_cell.shape[0]
    capacity = 2 * buffer_rows // devices
    slot_total = devices * capacity
    owner_ids = buffer_owner[:, 0]
    row_ids = jnp.arange(buffer_rows, dtype=jnp.int32)
    is_live = row_ids < buffer_count[0]
    one_hot = (owner_ids[:, None] == jnp.arange(devices, dtype=jnp.int32)[None, :]) & is_live[
        :, None
    ]
    one_hot_float = one_hot.astype(jnp.bfloat16)
    lower_mask = (row_ids[None, :] < row_ids[:, None]).astype(jnp.bfloat16)
    earlier = jnp.dot(lower_mask, one_hot_float, preferred_element_type=jnp.float32)
    ranks = jnp.sum(jnp.where(one_hot, earlier, 0.0), axis=1).astype(jnp.int32)
    target = jnp.where(is_live, owner_ids * capacity + ranks, slot_total)
    selector = (target[:, None] == jnp.arange(slot_total, dtype=jnp.int32)[None, :]).astype(
        jnp.float32
    )
    request = jnp.concatenate([buffer_frac, buffer_cell[None].astype(jnp.float32)], axis=0)
    outgoing = jnp.dot(
        request, selector, precision=lax.Precision.HIGHEST, preferred_element_type=jnp.float32
    )
    arrived = lax.all_to_all(outgoing, ("gx", "gy"), split_axis=1, concat_axis=1, tiled=True)
    returned = lax.all_to_all(
        answer_requests(fv_next, extra, arrived), ("gx", "gy"), split_axis=1, concat_axis=1, tiled=True
    )
    picked = lax.dot_general(
        returned,
        selector,
        (((1,), (1,)), ((), ())),
        precision=lax.Precision.HIGHEST,
        preferred_element_type=jnp.float32,
    )
    buffer_state = jnp.where(is_live[None, :], picked, 0.0)
    tiles_x, tiles_y, tile_slots = sph_press.shape
    tile_live = (
        jnp.arange(tile_slots, dtype=jnp.int32)[None, None, :] < tile_count[:, :, None]
    ).astype(jnp.float32)
    packed = jnp.concatenate([sph_offset, sph_vel, sph_press[None], tile_live[None]], axis=0)
    framed = padded_2(packed, (("gx", 1), ("gy", 2)), 1)
    own_tiles = packed.reshape(8, tiles_x * tiles_y, tile_slots)
    total = jnp.zeros((3, tiles_x * tiles_y, tile_slots), jnp.float32)
    for corner in range(9):
        step_x = corner // 3 - 1
        step_y = corner % 3 - 1
        other_tiles = framed[
            :, 1 + step_x : 1 + step_x + tiles_x, 1 + step_y : 1 + step_y + tiles_y
        ].reshape(8, tiles_x * tiles_y, tile_slots)
        total = total + pair_accel(own_tiles, other_tiles, float(step_x), float(step_y))
    sph_accel = (FORCE_SCALE * total * own_tiles[7][None]).reshape(3, tiles_x, tiles_y, tile_slots)
    return (fv_next, buffer_state, sph_accel)


def solution(mesh):
    return jax.shard_map(
        per_device,
        mesh=mesh,
        in_specs=(
            P(None, "gx", "gy", None),
            P(("gx", "gy"), None),
            P(("gx", "gy")),
            P(None, ("gx", "gy")),
            P(("gx", "gy")),
            P(None, "gx", "gy", None),
            P(None, "gx", "gy", None),
            P("gx", "gy", None),
            P("gx", "gy"),
        ),
        out_specs=(P(None, "gx", "gy", None), P(None, ("gx", "gy")), P(None, "gx", "gy", None)),
        check_vma=False,
    )
```

```python
import jax
import jax.numpy as jnp
from jax import lax
from jax.sharding import PartitionSpec as P

STEP_RATIO = 0.3
VISCOSITY = 0.02
FORCE_SCALE = 0.1


def padded_2(array, sides, width):
    for axis, dim in sides:
        count, length = (lax.axis_size(axis), array.shape[dim])
        up = [(i, (i + 1) % count) for i in range(count - 1)]
        down = [(j, i) for i, j in up]
        last = lax.slice_in_dim(array, length - width, length, axis=dim)
        leading = lax.slice_in_dim(array, 0, width, axis=dim)
        before = lax.ppermute(last, axis, up)
        after = lax.ppermute(leading, axis, down)
        array = jnp.concatenate([before, array, after], axis=dim)
    return array


def from_behind(array, axis, by):
    count = lax.axis_size(axis)
    pairs = [(i, i + by) for i in range(count) if 0 <= i + by < count]
    return lax.ppermute(array, axis, pairs)


def face_flux(left_side, right_side, normal):
    jump_term = right_side - left_side
    fluxes = [-0.5 * jump_term[channel] for channel in range(4)]
    fluxes[0] = fluxes[0] + 0.5 * (left_side[normal] + right_side[normal])
    fluxes[normal] = fluxes[normal] + 0.5 * (left_side[0] + right_side[0])
    return jnp.stack(fluxes)


def flux_step(padded):
    interior = padded[:, 1:-1, 1:-1, 1:-1]
    slab_rows = padded[:, :, 1:-1, 1:-1]
    across = face_flux(slab_rows[:, :-1], slab_rows[:, 1:], 1)
    change = across[:, 1:] - across[:, :-1]
    slab_rows = padded[:, 1:-1, :, 1:-1]
    across = face_flux(slab_rows[:, :, :-1], slab_rows[:, :, 1:], 2)
    change = change + (across[:, :, 1:] - across[:, :, :-1])
    slab_rows = padded[:, 1:-1, 1:-1, :]
    across = face_flux(slab_rows[:, :, :, :-1], slab_rows[:, :, :, 1:], 3)
    change = change + (across[:, :, :, 1:] - across[:, :, :, :-1])
    return interior - STEP_RATIO * change


def flux_sweep(state, x_lo, x_hi, y_lo, y_hi):
    rim = ((0, 0), (0, 0), (1, 1), (0, 0))
    middle = jnp.concatenate([y_lo, state, y_hi], axis=2)
    bordered = jnp.concatenate([jnp.pad(x_lo, rim), middle, jnp.pad(x_hi, rim)], axis=1)
    return flux_step(jnp.pad(bordered, ((0, 0), (0, 0), (0, 0), (1, 1))))


def from_diagonal(array):
    count_x = lax.axis_size("gx")
    count_y = lax.axis_size("gy")
    pairs = [
        ((i + 1) * count_y + j + 1, i * count_y + j)
        for i in range(count_x - 1)
        for j in range(count_y - 1)
    ]
    return lax.ppermute(array, ("gx", "gy"), pairs)


def answer_requests(main, extra, arrived):
    channels, cells_x, cells_y, cells_z = main.shape
    count = arrived.shape[1]
    cell_index = arrived[3].astype(jnp.int32)
    base_x = cell_index // (cells_y * cells_z)
    base_y = cell_index // cells_z % cells_y
    base_z = cell_index % cells_z
    frac_x, frac_y, frac_z = arrived[0], arrived[1], arrived[2]
    z_ids = lax.broadcasted_iota(jnp.int32, (cells_z, count), 0)
    z_weight = jnp.where(z_ids == base_z[None, :], 1.0 - frac_z[None, :], 0.0) + jnp.where(
        z_ids == base_z[None, :] + 1, frac_z[None, :], 0.0
    )

    def contract(part):
        return lax.dot_general(
            part,
            z_weight,
            (((part.ndim - 1,), (0,)), ((), ())),
            precision=lax.Precision.HIGH,
            preferred_element_type=jnp.float32,
        )

    x_ids = lax.broadcasted_iota(jnp.int32, (cells_x, count), 0)
    y_ids = lax.broadcasted_iota(jnp.int32, (cells_y, count), 0)
    weight_x = jnp.where(x_ids == base_x, 1.0 - frac_x, 0.0) + jnp.where(x_ids == base_x + 1, frac_x, 0.0)
    weight_y = jnp.where(y_ids == base_y, 1.0 - frac_y, 0.0) + jnp.where(y_ids == base_y + 1, frac_y, 0.0)
    edge_x = jnp.where(base_x + 1 == cells_x, frac_x, 0.0)
    edge_y = jnp.where(base_y + 1 == cells_y, frac_y, 0.0)
    weight_main = weight_x[:, None, :] * weight_y[None, :, :]
    weight_extra = jnp.concatenate(
        [edge_x[None] * weight_y, weight_x * edge_y[None], (edge_x * edge_y)[None]], axis=0
    )
    values = jnp.sum(contract(main) * weight_main[None], axis=(1, 2))
    return values + jnp.sum(contract(extra) * weight_extra[None], axis=1)


def pair_accel(own_tiles, other_tiles, shift_x, shift_y):
    separation_x = own_tiles[0][:, :, None] - other_tiles[0][:, None, :] - shift_x
    separation_y = own_tiles[1][:, :, None] - other_tiles[1][:, None, :] - shift_y
    separation_z = own_tiles[2][:, :, None] - other_tiles[2][:, None, :]
    distance = jnp.sqrt(
        separation_x * separation_x + separation_y * separation_y + separation_z * separation_z
    )
    closeness = jnp.maximum(1.0 - distance, 0.0)
    weight = 20.0 * closeness * closeness * closeness * other_tiles[7][:, None, :]
    push_term = (own_tiles[6][:, :, None] + other_tiles[6][:, None, :]) * weight
    weight_total = jnp.sum(weight, axis=-1)
    result = []
    for channel, separation in enumerate((separation_x, separation_y, separation_z)):
        drag_term = (
            jnp.sum(weight * other_tiles[3 + channel][:, None, :], axis=-1)
            - weight_total * own_tiles[3 + channel]
        )
        result.append(jnp.sum(push_term * separation, axis=-1) + VISCOSITY * drag_term)
    return jnp.stack(result)


def per_device(
    fv_state,
    buffer_owner,
    buffer_cell,
    buffer_frac,
    buffer_count,
    sph_offset,
    sph_vel,
    sph_press,
    tile_count,
):
    grid_x = lax.axis_size("gx")
    grid_y = lax.axis_size("gy")
    x_lo = from_behind(fv_state[:, -1:], "gx", 1)
    x_hi = from_behind(fv_state[:, :1], "gx", -1)
    y_lo = from_behind(fv_state[:, :, -1:], "gy", 1)
    y_hi = from_behind(fv_state[:, :, :1], "gy", -1)
    fv_next = flux_sweep(fv_state, x_lo, x_hi, y_lo, y_hi)
    row_next = from_behind(fv_next[:, 0], "gx", -1)
    column_next = from_behind(fv_next[:, :, 0], "gy", -1)
    corner_next = from_diagonal(fv_next[:, 0, 0])
    extra = jnp.concatenate([row_next, column_next, corner_next[:, None]], axis=1)
    devices = grid_x * grid_y
    buffer_rows = buffer_cell.shape[0]
    capacity = 2 * buffer_rows // devices
    slot_total = devices * capacity
    owner_ids = buffer_owner[:, 0]
    row_ids = jnp.arange(buffer_rows, dtype=jnp.int32)
    is_live = row_ids < buffer_count[0]
    one_hot = (owner_ids[:, None] == jnp.arange(devices, dtype=jnp.int32)[None, :]) & is_live[
        :, None
    ]
    one_hot_float = one_hot.astype(jnp.bfloat16)
    lower_mask = (row_ids[None, :] < row_ids[:, None]).astype(jnp.bfloat16)
    earlier = jnp.dot(lower_mask, one_hot_float, preferred_element_type=jnp.float32)
    ranks = jnp.sum(jnp.where(one_hot, earlier, 0.0), axis=1).astype(jnp.int32)
    target = jnp.where(is_live, owner_ids * capacity + ranks, slot_total)
    selector = (target[:, None] == jnp.arange(slot_total, dtype=jnp.int32)[None, :]).astype(
        jnp.float32
    )
    request = jnp.concatenate([buffer_frac, buffer_cell[None].astype(jnp.float32)], axis=0)
    outgoing = jnp.dot(
        request, selector, precision=lax.Precision.HIGHEST, preferred_element_type=jnp.float32
    )
    arrived = lax.all_to_all(outgoing, ("gx", "gy"), split_axis=1, concat_axis=1, tiled=True)
    returned = lax.all_to_all(
        answer_requests(fv_next, extra, arrived), ("gx", "gy"), split_axis=1, concat_axis=1, tiled=True
    )
    picked = lax.dot_general(
        returned,
        selector,
        (((1,), (1,)), ((), ())),
        precision=lax.Precision.HIGHEST,
        preferred_element_type=jnp.float32,
    )
    buffer_state = jnp.where(is_live[None, :], picked, 0.0)
    tiles_x, tiles_y, tile_slots = sph_press.shape
    tile_live = (
        jnp.arange(tile_slots, dtype=jnp.int32)[None, None, :] < tile_count[:, :, None]
    ).astype(jnp.float32)
    packed = jnp.concatenate([sph_offset, sph_vel, sph_press[None], tile_live[None]], axis=0)
    framed = padded_2(packed, (("gx", 1), ("gy", 2)), 1)
    own_tiles = packed.reshape(8, tiles_x * tiles_y, tile_slots)
    total = jnp.zeros((3, tiles_x * tiles_y, tile_slots), jnp.float32)
    for corner in range(9):
        step_x = corner // 3 - 1
        step_y = corner % 3 - 1
        other_tiles = framed[
            :, 1 + step_x : 1 + step_x + tiles_x, 1 + step_y : 1 + step_y + tiles_y
        ].reshape(8, tiles_x * tiles_y, tile_slots)
        total = total + pair_accel(own_tiles, other_tiles, float(step_x), float(step_y))
    sph_accel = (FORCE_SCALE * total * own_tiles[7][None]).reshape(3, tiles_x, tiles_y, tile_slots)
    return (fv_next, buffer_state, sph_accel)


def solution(mesh):
    return jax.shard_map(
        per_device,
        mesh=mesh,
        in_specs=(
            P(None, "gx", "gy", None),
            P(("gx", "gy"), None),
            P(("gx", "gy")),
            P(None, ("gx", "gy")),
            P(("gx", "gy")),
            P(None, "gx", "gy", None),
            P(None, "gx", "gy", None),
            P("gx", "gy", None),
            P("gx", "gy"),
        ),
        out_specs=(P(None, "gx", "gy", None), P(None, ("gx", "gy")), P(None, "gx", "gy", None)),
        check_vma=False,
    )
```

```python
import jax
import jax.numpy as jnp
from jax import lax
from jax.experimental import pallas as pl
from jax.experimental.pallas import tpu as pltpu
from jax.sharding import PartitionSpec as P

STEP_RATIO = 0.3
VISCOSITY = 0.02
FORCE_SCALE = 0.1


def padded_2(array, sides, width):
    for axis, dim in sides:
        count, length = (lax.axis_size(axis), array.shape[dim])
        up = [(i, (i + 1) % count) for i in range(count - 1)]
        down = [(j, i) for i, j in up]
        last = lax.slice_in_dim(array, length - width, length, axis=dim)
        leading = lax.slice_in_dim(array, 0, width, axis=dim)
        before = lax.ppermute(last, axis, up)
        after = lax.ppermute(leading, axis, down)
        array = jnp.concatenate([before, array, after], axis=dim)
    return array


def from_behind(array, axis, by):
    count = lax.axis_size(axis)
    pairs = [(i, i + by) for i in range(count) if 0 <= i + by < count]
    return lax.ppermute(array, axis, pairs)


def face_flux(left_side, right_side, normal):
    jump_term = right_side - left_side
    fluxes = [-0.5 * jump_term[channel] for channel in range(4)]
    fluxes[0] = fluxes[0] + 0.5 * (left_side[normal] + right_side[normal])
    fluxes[normal] = fluxes[normal] + 0.5 * (left_side[0] + right_side[0])
    return jnp.stack(fluxes)


def flux_kernel(state_ref, x_lo_ref, x_hi_ref, y_lo_ref, y_hi_ref, out_ref):
    channels, rows, cols, depth = state_ref.shape
    col_ids = lax.broadcasted_iota(jnp.int32, (cols, depth), 0)
    lane_ids = lax.broadcasted_iota(jnp.int32, (cols, depth), 1)
    for x in range(rows):
        centre = [state_ref[c, x] for c in range(channels)]
        ahead = [state_ref[c, x + 1] if x + 1 < rows else x_hi_ref[c, 0] for c in range(channels)]
        behind = [state_ref[c, x - 1] if x > 0 else x_lo_ref[c, 0] for c in range(channels)]
        up_y = [
            jnp.where(col_ids == cols - 1, y_hi_ref[c, x], pltpu.roll(centre[c], cols - 1, 0))
            for c in range(channels)
        ]
        down_y = [
            jnp.where(col_ids == 0, y_lo_ref[c, x], pltpu.roll(centre[c], 1, 0))
            for c in range(channels)
        ]
        up_z = [
            jnp.where(lane_ids == depth - 1, 0.0, pltpu.roll(centre[c], depth - 1, 1))
            for c in range(channels)
        ]
        down_z = [jnp.where(lane_ids == 0, 0.0, pltpu.roll(centre[c], 1, 1)) for c in range(channels)]
        change = None
        for normal, (lower, upper) in ((1, (behind, ahead)), (2, (down_y, up_y)), (3, (down_z, up_z))):
            high = face_flux_list(centre, upper, normal)
            low = face_flux_list(lower, centre, normal)
            step = [high[c] - low[c] for c in range(channels)]
            change = step if change is None else [change[c] + step[c] for c in range(channels)]
        for c in range(channels):
            out_ref[c, x] = centre[c] - STEP_RATIO * change[c]


def face_flux_list(left_side, right_side, normal):
    fluxes = [-0.5 * (right_side[c] - left_side[c]) for c in range(len(left_side))]
    fluxes[0] = fluxes[0] + 0.5 * (left_side[normal] + right_side[normal])
    fluxes[normal] = fluxes[normal] + 0.5 * (left_side[0] + right_side[0])
    return fluxes


def flux_sweep(state, x_lo, x_hi, y_lo, y_hi):
    return pl.pallas_call(
        flux_kernel,
        out_shape=jax.ShapeDtypeStruct(state.shape, state.dtype),
    )(state, x_lo, x_hi, y_lo, y_hi)


def from_diagonal(array):
    count_x = lax.axis_size("gx")
    count_y = lax.axis_size("gy")
    pairs = [
        ((i + 1) * count_y + j + 1, i * count_y + j)
        for i in range(count_x - 1)
        for j in range(count_y - 1)
    ]
    return lax.ppermute(array, ("gx", "gy"), pairs)


def answer_requests(main, extra, arrived):
    channels, cells_x, cells_y, cells_z = main.shape
    count = arrived.shape[1]
    cell_index = arrived[3].astype(jnp.int32)
    base_x = cell_index // (cells_y * cells_z)
    base_y = cell_index // cells_z % cells_y
    base_z = cell_index % cells_z
    frac_x, frac_y, frac_z = arrived[0], arrived[1], arrived[2]
    z_ids = lax.broadcasted_iota(jnp.int32, (cells_z, count), 0)
    z_weight = jnp.where(z_ids == base_z[None, :], 1.0 - frac_z[None, :], 0.0) + jnp.where(
        z_ids == base_z[None, :] + 1, frac_z[None, :], 0.0
    )

    def contract(part):
        return lax.dot_general(
            part,
            z_weight,
            (((part.ndim - 1,), (0,)), ((), ())),
            precision=lax.Precision.HIGH,
            preferred_element_type=jnp.float32,
        )

    x_ids = lax.broadcasted_iota(jnp.int32, (cells_x, count), 0)
    y_ids = lax.broadcasted_iota(jnp.int32, (cells_y, count), 0)
    weight_x = jnp.where(x_ids == base_x, 1.0 - frac_x, 0.0) + jnp.where(x_ids == base_x + 1, frac_x, 0.0)
    weight_y = jnp.where(y_ids == base_y, 1.0 - frac_y, 0.0) + jnp.where(y_ids == base_y + 1, frac_y, 0.0)
    edge_x = jnp.where(base_x + 1 == cells_x, frac_x, 0.0)
    edge_y = jnp.where(base_y + 1 == cells_y, frac_y, 0.0)
    weight_main = weight_x[:, None, :] * weight_y[None, :, :]
    weight_extra = jnp.concatenate(
        [edge_x[None] * weight_y, weight_x * edge_y[None], (edge_x * edge_y)[None]], axis=0
    )
    values = jnp.sum(contract(main) * weight_main[None], axis=(1, 2))
    return values + jnp.sum(contract(extra) * weight_extra[None], axis=1)


def pair_accel(own_tiles, other_tiles, shift_x, shift_y):
    separation_x = own_tiles[0][:, :, None] - other_tiles[0][:, None, :] - shift_x
    separation_y = own_tiles[1][:, :, None] - other_tiles[1][:, None, :] - shift_y
    separation_z = own_tiles[2][:, :, None] - other_tiles[2][:, None, :]
    distance = jnp.sqrt(
        separation_x * separation_x + separation_y * separation_y + separation_z * separation_z
    )
    closeness = jnp.maximum(1.0 - distance, 0.0)
    weight = 20.0 * closeness * closeness * closeness * other_tiles[7][:, None, :]
    push_term = (own_tiles[6][:, :, None] + other_tiles[6][:, None, :]) * weight
    weight_total = jnp.sum(weight, axis=-1)
    result = []
    for channel, separation in enumerate((separation_x, separation_y, separation_z)):
        drag_term = (
            jnp.sum(weight * other_tiles[3 + channel][:, None, :], axis=-1)
            - weight_total * own_tiles[3 + channel]
        )
        result.append(jnp.sum(push_term * separation, axis=-1) + VISCOSITY * drag_term)
    return jnp.stack(result)


def per_device(
    fv_state,
    buffer_owner,
    buffer_cell,
    buffer_frac,
    buffer_count,
    sph_offset,
    sph_vel,
    sph_press,
    tile_count,
):
    grid_x = lax.axis_size("gx")
    grid_y = lax.axis_size("gy")
    x_lo = from_behind(fv_state[:, -1:], "gx", 1)
    x_hi = from_behind(fv_state[:, :1], "gx", -1)
    y_lo = from_behind(fv_state[:, :, -1:], "gy", 1)
    y_hi = from_behind(fv_state[:, :, :1], "gy", -1)
    fv_next = flux_sweep(fv_state, x_lo, x_hi, y_lo, y_hi)
    row_next = from_behind(fv_next[:, 0], "gx", -1)
    column_next = from_behind(fv_next[:, :, 0], "gy", -1)
    corner_next = from_diagonal(fv_next[:, 0, 0])
    extra = jnp.concatenate([row_next, column_next, corner_next[:, None]], axis=1)
    devices = grid_x * grid_y
    buffer_rows = buffer_cell.shape[0]
    capacity = 2 * buffer_rows // devices
    slot_total = devices * capacity
    owner_ids = buffer_owner[:, 0]
    row_ids = jnp.arange(buffer_rows, dtype=jnp.int32)
    is_live = row_ids < buffer_count[0]
    one_hot = (owner_ids[:, None] == jnp.arange(devices, dtype=jnp.int32)[None, :]) & is_live[
        :, None
    ]
    one_hot_float = one_hot.astype(jnp.bfloat16)
    lower_mask = (row_ids[None, :] < row_ids[:, None]).astype(jnp.bfloat16)
    earlier = jnp.dot(lower_mask, one_hot_float, preferred_element_type=jnp.float32)
    ranks = jnp.sum(jnp.where(one_hot, earlier, 0.0), axis=1).astype(jnp.int32)
    target = jnp.where(is_live, owner_ids * capacity + ranks, slot_total)
    selector = (target[:, None] == jnp.arange(slot_total, dtype=jnp.int32)[None, :]).astype(
        jnp.float32
    )
    request = jnp.concatenate([buffer_frac, buffer_cell[None].astype(jnp.float32)], axis=0)
    outgoing = jnp.dot(
        request, selector, precision=lax.Precision.HIGHEST, preferred_element_type=jnp.float32
    )
    arrived = lax.all_to_all(outgoing, ("gx", "gy"), split_axis=1, concat_axis=1, tiled=True)
    returned = lax.all_to_all(
        answer_requests(fv_next, extra, arrived), ("gx", "gy"), split_axis=1, concat_axis=1, tiled=True
    )
    picked = lax.dot_general(
        returned,
        selector,
        (((1,), (1,)), ((), ())),
        precision=lax.Precision.HIGHEST,
        preferred_element_type=jnp.float32,
    )
    buffer_state = jnp.where(is_live[None, :], picked, 0.0)
    tiles_x, tiles_y, tile_slots = sph_press.shape
    tile_live = (
        jnp.arange(tile_slots, dtype=jnp.int32)[None, None, :] < tile_count[:, :, None]
    ).astype(jnp.float32)
    packed = jnp.concatenate([sph_offset, sph_vel, sph_press[None], tile_live[None]], axis=0)
    framed = padded_2(packed, (("gx", 1), ("gy", 2)), 1)
    own_tiles = packed.reshape(8, tiles_x * tiles_y, tile_slots)
    total = jnp.zeros((3, tiles_x * tiles_y, tile_slots), jnp.float32)
    for corner in range(9):
        step_x = corner // 3 - 1
        step_y = corner % 3 - 1
        other_tiles = framed[
            :, 1 + step_x : 1 + step_x + tiles_x, 1 + step_y : 1 + step_y + tiles_y
        ].reshape(8, tiles_x * tiles_y, tile_slots)
        total = total + pair_accel(own_tiles, other_tiles, float(step_x), float(step_y))
    sph_accel = (FORCE_SCALE * total * own_tiles[7][None]).reshape(3, tiles_x, tiles_y, tile_slots)
    return (fv_next, buffer_state, sph_accel)


def solution(mesh):
    return jax.shard_map(
        per_device,
        mesh=mesh,
        in_specs=(
            P(None, "gx", "gy", None),
            P(("gx", "gy"), None),
            P(("gx", "gy")),
            P(None, ("gx", "gy")),
            P(("gx", "gy")),
            P(None, "gx", "gy", None),
            P(None, "gx", "gy", None),
            P("gx", "gy", None),
            P("gx", "gy"),
        ),
        out_specs=(P(None, "gx", "gy", None), P(None, ("gx", "gy")), P(None, "gx", "gy", None)),
        check_vma=False,
    )
```

```python
import jax
import jax.numpy as jnp
from jax import lax
from jax.experimental import pallas as pl
from jax.experimental.pallas import tpu as pltpu
from jax.sharding import PartitionSpec as P

STEP_RATIO = 0.3
VISCOSITY = 0.02
FORCE_SCALE = 0.1


def padded_2(array, sides, width):
    for axis, dim in sides:
        count, length = (lax.axis_size(axis), array.shape[dim])
        up = [(i, (i + 1) % count) for i in range(count - 1)]
        down = [(j, i) for i, j in up]
        last = lax.slice_in_dim(array, length - width, length, axis=dim)
        leading = lax.slice_in_dim(array, 0, width, axis=dim)
        before = lax.ppermute(last, axis, up)
        after = lax.ppermute(leading, axis, down)
        array = jnp.concatenate([before, array, after], axis=dim)
    return array


def from_behind(array, axis, by):
    count = lax.axis_size(axis)
    pairs = [(i, i + by) for i in range(count) if 0 <= i + by < count]
    return lax.ppermute(array, axis, pairs)


def face_flux(left_side, right_side, normal):
    jump_term = right_side - left_side
    fluxes = [-0.5 * jump_term[channel] for channel in range(4)]
    fluxes[0] = fluxes[0] + 0.5 * (left_side[normal] + right_side[normal])
    fluxes[normal] = fluxes[normal] + 0.5 * (left_side[0] + right_side[0])
    return jnp.stack(fluxes)


def flux_kernel(state_ref, x_lo_ref, x_hi_ref, y_lo_ref, y_hi_ref, out_ref):
    channels, rows, cols, depth = state_ref.shape
    col_ids = lax.broadcasted_iota(jnp.int32, (cols, depth), 0)
    lane_ids = lax.broadcasted_iota(jnp.int32, (cols, depth), 1)
    for x in range(rows):
        centre = [state_ref[c, x] for c in range(channels)]
        ahead = [state_ref[c, x + 1] if x + 1 < rows else x_hi_ref[c, 0] for c in range(channels)]
        behind = [state_ref[c, x - 1] if x > 0 else x_lo_ref[c, 0] for c in range(channels)]
        up_y = [
            jnp.where(col_ids == cols - 1, y_hi_ref[c, x], pltpu.roll(centre[c], cols - 1, 0))
            for c in range(channels)
        ]
        down_y = [
            jnp.where(col_ids == 0, y_lo_ref[c, x], pltpu.roll(centre[c], 1, 0))
            for c in range(channels)
        ]
        up_z = [
            jnp.where(lane_ids == depth - 1, 0.0, pltpu.roll(centre[c], depth - 1, 1))
            for c in range(channels)
        ]
        down_z = [jnp.where(lane_ids == 0, 0.0, pltpu.roll(centre[c], 1, 1)) for c in range(channels)]
        change = None
        for normal, (lower, upper) in ((1, (behind, ahead)), (2, (down_y, up_y)), (3, (down_z, up_z))):
            high = face_flux_list(centre, upper, normal)
            low = face_flux_list(lower, centre, normal)
            step = [high[c] - low[c] for c in range(channels)]
            change = step if change is None else [change[c] + step[c] for c in range(channels)]
        for c in range(channels):
            out_ref[c, x] = centre[c] - STEP_RATIO * change[c]


def face_flux_list(left_side, right_side, normal):
    fluxes = [-0.5 * (right_side[c] - left_side[c]) for c in range(len(left_side))]
    fluxes[0] = fluxes[0] + 0.5 * (left_side[normal] + right_side[normal])
    fluxes[normal] = fluxes[normal] + 0.5 * (left_side[0] + right_side[0])
    return fluxes


def flux_sweep(state, x_lo, x_hi, y_lo, y_hi):
    return pl.pallas_call(
        flux_kernel,
        out_shape=jax.ShapeDtypeStruct(state.shape, state.dtype),
    )(state, x_lo, x_hi, y_lo, y_hi)


def from_diagonal(array):
    count_x = lax.axis_size("gx")
    count_y = lax.axis_size("gy")
    pairs = [
        ((i + 1) * count_y + j + 1, i * count_y + j)
        for i in range(count_x - 1)
        for j in range(count_y - 1)
    ]
    return lax.ppermute(array, ("gx", "gy"), pairs)


def answer_requests(main, extra, arrived):
    channels, cells_x, cells_y, cells_z = main.shape
    count = arrived.shape[1]
    cell_index = arrived[3].astype(jnp.int32)
    base_x = cell_index // (cells_y * cells_z)
    base_y = cell_index // cells_z % cells_y
    base_z = cell_index % cells_z
    frac_x, frac_y, frac_z = arrived[0], arrived[1], arrived[2]
    z_ids = lax.broadcasted_iota(jnp.int32, (cells_z, count), 0)
    z_weight = jnp.where(z_ids == base_z[None, :], 1.0 - frac_z[None, :], 0.0) + jnp.where(
        z_ids == base_z[None, :] + 1, frac_z[None, :], 0.0
    )

    def contract(part):
        return lax.dot_general(
            part,
            z_weight,
            (((part.ndim - 1,), (0,)), ((), ())),
            precision=lax.Precision.HIGH,
            preferred_element_type=jnp.float32,
        )

    x_ids = lax.broadcasted_iota(jnp.int32, (cells_x, count), 0)
    y_ids = lax.broadcasted_iota(jnp.int32, (cells_y, count), 0)
    weight_x = jnp.where(x_ids == base_x, 1.0 - frac_x, 0.0) + jnp.where(x_ids == base_x + 1, frac_x, 0.0)
    weight_y = jnp.where(y_ids == base_y, 1.0 - frac_y, 0.0) + jnp.where(y_ids == base_y + 1, frac_y, 0.0)
    edge_x = jnp.where(base_x + 1 == cells_x, frac_x, 0.0)
    edge_y = jnp.where(base_y + 1 == cells_y, frac_y, 0.0)
    weight_main = weight_x[:, None, :] * weight_y[None, :, :]
    weight_extra = jnp.concatenate(
        [edge_x[None] * weight_y, weight_x * edge_y[None], (edge_x * edge_y)[None]], axis=0
    )
    values = jnp.sum(contract(main) * weight_main[None], axis=(1, 2))
    return values + jnp.sum(contract(extra) * weight_extra[None], axis=1)


def pair_sums(own_tiles, other_tiles):
    separations = [own_tiles[c][:, None, :] - other_tiles[c][:, :, None] for c in range(3)]
    distance = jnp.sqrt(sum(separation * separation for separation in separations))
    closeness = jnp.maximum(1.0 - distance, 0.0)
    weight = 20.0 * closeness * closeness * closeness * other_tiles[7][:, :, None]
    push_term = (own_tiles[6][:, None, :] + other_tiles[6][:, :, None]) * weight
    weight_total = jnp.sum(weight, axis=1)
    result = []
    for channel, separation in enumerate(separations):
        drag_term = (
            jnp.sum(weight * other_tiles[3 + channel][:, :, None], axis=1)
            - weight_total * own_tiles[3 + channel]
        )
        result.append(jnp.sum(push_term * separation, axis=1) + VISCOSITY * drag_term)
    return jnp.stack(result)


def per_device(
    fv_state,
    buffer_owner,
    buffer_cell,
    buffer_frac,
    buffer_count,
    sph_offset,
    sph_vel,
    sph_press,
    tile_count,
):
    grid_x = lax.axis_size("gx")
    grid_y = lax.axis_size("gy")
    x_lo = from_behind(fv_state[:, -1:], "gx", 1)
    x_hi = from_behind(fv_state[:, :1], "gx", -1)
    y_lo = from_behind(fv_state[:, :, -1:], "gy", 1)
    y_hi = from_behind(fv_state[:, :, :1], "gy", -1)
    fv_next = flux_sweep(fv_state, x_lo, x_hi, y_lo, y_hi)
    row_next = from_behind(fv_next[:, 0], "gx", -1)
    column_next = from_behind(fv_next[:, :, 0], "gy", -1)
    corner_next = from_diagonal(fv_next[:, 0, 0])
    extra = jnp.concatenate([row_next, column_next, corner_next[:, None]], axis=1)
    devices = grid_x * grid_y
    buffer_rows = buffer_cell.shape[0]
    capacity = 2 * buffer_rows // devices
    slot_total = devices * capacity
    owner_ids = buffer_owner[:, 0]
    row_ids = jnp.arange(buffer_rows, dtype=jnp.int32)
    is_live = row_ids < buffer_count[0]
    one_hot = (owner_ids[:, None] == jnp.arange(devices, dtype=jnp.int32)[None, :]) & is_live[
        :, None
    ]
    one_hot_float = one_hot.astype(jnp.bfloat16)
    lower_mask = (row_ids[None, :] < row_ids[:, None]).astype(jnp.bfloat16)
    earlier = jnp.dot(lower_mask, one_hot_float, preferred_element_type=jnp.float32)
    ranks = jnp.sum(jnp.where(one_hot, earlier, 0.0), axis=1).astype(jnp.int32)
    target = jnp.where(is_live, owner_ids * capacity + ranks, slot_total)
    selector = (target[:, None] == jnp.arange(slot_total, dtype=jnp.int32)[None, :]).astype(
        jnp.float32
    )
    request = jnp.concatenate([buffer_frac, buffer_cell[None].astype(jnp.float32)], axis=0)
    outgoing = jnp.dot(
        request, selector, precision=lax.Precision.HIGHEST, preferred_element_type=jnp.float32
    )
    arrived = lax.all_to_all(outgoing, ("gx", "gy"), split_axis=1, concat_axis=1, tiled=True)
    returned = lax.all_to_all(
        answer_requests(fv_next, extra, arrived), ("gx", "gy"), split_axis=1, concat_axis=1, tiled=True
    )
    picked = lax.dot_general(
        returned,
        selector,
        (((1,), (1,)), ((), ())),
        precision=lax.Precision.HIGHEST,
        preferred_element_type=jnp.float32,
    )
    buffer_state = jnp.where(is_live[None, :], picked, 0.0)
    tiles_x, tiles_y, tile_slots = sph_press.shape
    tile_live = (
        jnp.arange(tile_slots, dtype=jnp.int32)[None, None, :] < tile_count[:, :, None]
    ).astype(jnp.float32)
    packed = jnp.concatenate([sph_offset, sph_vel, sph_press[None], tile_live[None]], axis=0)
    framed = padded_2(packed, (("gx", 1), ("gy", 2)), 1)
    own_tiles = packed.reshape(8, tiles_x * tiles_y, tile_slots)
    neighbours = []
    for corner in range(9):
        step_x = corner // 3 - 1
        step_y = corner % 3 - 1
        window = framed[:, 1 + step_x : 1 + step_x + tiles_x, 1 + step_y : 1 + step_y + tiles_y]
        shift = jnp.array([step_x, step_y, 0, 0, 0, 0, 0, 0], jnp.float32)[:, None, None, None]
        neighbours.append(window + shift)
    other_tiles = jnp.stack(neighbours, axis=3).reshape(8, tiles_x * tiles_y, 9 * tile_slots)
    total = pair_sums(own_tiles, other_tiles)
    sph_accel = (FORCE_SCALE * total * own_tiles[7][None]).reshape(3, tiles_x, tiles_y, tile_slots)
    return (fv_next, buffer_state, sph_accel)


def solution(mesh):
    return jax.shard_map(
        per_device,
        mesh=mesh,
        in_specs=(
            P(None, "gx", "gy", None),
            P(("gx", "gy"), None),
            P(("gx", "gy")),
            P(None, ("gx", "gy")),
            P(("gx", "gy")),
            P(None, "gx", "gy", None),
            P(None, "gx", "gy", None),
            P("gx", "gy", None),
            P("gx", "gy"),
        ),
        out_specs=(P(None, "gx", "gy", None), P(None, ("gx", "gy")), P(None, "gx", "gy", None)),
        check_vma=False,
    )
```

```python
import jax
import jax.numpy as jnp
from jax import lax
from jax.experimental import pallas as pl
from jax.experimental.pallas import tpu as pltpu
from jax.sharding import PartitionSpec as P

STEP_RATIO = 0.3
VISCOSITY = 0.02
FORCE_SCALE = 0.1


def padded_2(array, sides, width):
    for axis, dim in sides:
        count, length = (lax.axis_size(axis), array.shape[dim])
        up = [(i, (i + 1) % count) for i in range(count - 1)]
        down = [(j, i) for i, j in up]
        last = lax.slice_in_dim(array, length - width, length, axis=dim)
        leading = lax.slice_in_dim(array, 0, width, axis=dim)
        before = lax.ppermute(last, axis, up)
        after = lax.ppermute(leading, axis, down)
        array = jnp.concatenate([before, array, after], axis=dim)
    return array


def from_behind(array, axis, by):
    count = lax.axis_size(axis)
    pairs = [(i, i + by) for i in range(count) if 0 <= i + by < count]
    return lax.ppermute(array, axis, pairs)


def face_flux(left_side, right_side, normal):
    jump_term = right_side - left_side
    fluxes = [-0.5 * jump_term[channel] for channel in range(4)]
    fluxes[0] = fluxes[0] + 0.5 * (left_side[normal] + right_side[normal])
    fluxes[normal] = fluxes[normal] + 0.5 * (left_side[0] + right_side[0])
    return jnp.stack(fluxes)


def flux_kernel(state_ref, x_lo_ref, x_hi_ref, y_lo_ref, y_hi_ref, out_ref, row_ref, column_ref, corner_ref):
    channels, rows, cols, depth = state_ref.shape
    col_ids = lax.broadcasted_iota(jnp.int32, (cols, depth), 0)
    lane_ids = lax.broadcasted_iota(jnp.int32, (cols, depth), 1)
    for x in range(rows):
        centre = [state_ref[c, x] for c in range(channels)]
        ahead = [state_ref[c, x + 1] if x + 1 < rows else x_hi_ref[c, 0] for c in range(channels)]
        behind = [state_ref[c, x - 1] if x > 0 else x_lo_ref[c, 0] for c in range(channels)]
        up_y = [
            jnp.where(col_ids == cols - 1, y_hi_ref[c, x], pltpu.roll(centre[c], cols - 1, 0))
            for c in range(channels)
        ]
        down_y = [
            jnp.where(col_ids == 0, y_lo_ref[c, x], pltpu.roll(centre[c], 1, 0))
            for c in range(channels)
        ]
        up_z = [
            jnp.where(lane_ids == depth - 1, 0.0, pltpu.roll(centre[c], depth - 1, 1))
            for c in range(channels)
        ]
        down_z = [jnp.where(lane_ids == 0, 0.0, pltpu.roll(centre[c], 1, 1)) for c in range(channels)]
        change = None
        for normal, (lower, upper) in ((1, (behind, ahead)), (2, (down_y, up_y)), (3, (down_z, up_z))):
            high = face_flux_list(centre, upper, normal)
            low = face_flux_list(lower, centre, normal)
            step = [high[c] - low[c] for c in range(channels)]
            change = step if change is None else [change[c] + step[c] for c in range(channels)]
        for c in range(channels):
            result = centre[c] - STEP_RATIO * change[c]
            out_ref[c, x] = result
            column_ref[c, x : x + 1] = result[0:1]
            if x == 0:
                row_ref[c] = result
                corner_ref[c : c + 1] = result[0:1]


def face_flux_list(left_side, right_side, normal):
    fluxes = [-0.5 * (right_side[c] - left_side[c]) for c in range(len(left_side))]
    fluxes[0] = fluxes[0] + 0.5 * (left_side[normal] + right_side[normal])
    fluxes[normal] = fluxes[normal] + 0.5 * (left_side[0] + right_side[0])
    return fluxes


def flux_sweep(state, x_lo, x_hi, y_lo, y_hi):
    channels, rows, cols, depth = state.shape
    return pl.pallas_call(
        flux_kernel,
        out_shape=(
            jax.ShapeDtypeStruct(state.shape, state.dtype),
            jax.ShapeDtypeStruct((channels, cols, depth), state.dtype),
            jax.ShapeDtypeStruct((channels, rows, depth), state.dtype),
            jax.ShapeDtypeStruct((channels, depth), state.dtype),
        ),
    )(state, x_lo, x_hi, y_lo, y_hi)


def from_diagonal(array):
    count_x = lax.axis_size("gx")
    count_y = lax.axis_size("gy")
    pairs = [
        ((i + 1) * count_y + j + 1, i * count_y + j)
        for i in range(count_x - 1)
        for j in range(count_y - 1)
    ]
    return lax.ppermute(array, ("gx", "gy"), pairs)


def answer_requests(main, extra, arrived):
    channels, cells_x, cells_y, cells_z = main.shape
    count = arrived.shape[1]
    cell_index = arrived[3].astype(jnp.int32)
    base_x = cell_index // (cells_y * cells_z)
    base_y = cell_index // cells_z % cells_y
    base_z = cell_index % cells_z
    frac_x, frac_y, frac_z = arrived[0], arrived[1], arrived[2]
    z_ids = lax.broadcasted_iota(jnp.int32, (cells_z, count), 0)
    z_weight = jnp.where(z_ids == base_z[None, :], 1.0 - frac_z[None, :], 0.0) + jnp.where(
        z_ids == base_z[None, :] + 1, frac_z[None, :], 0.0
    )

    def contract(part):
        return lax.dot_general(
            part,
            z_weight,
            (((part.ndim - 1,), (0,)), ((), ())),
            precision=lax.Precision.HIGH,
            preferred_element_type=jnp.float32,
        )

    x_ids = lax.broadcasted_iota(jnp.int32, (cells_x, count), 0)
    y_ids = lax.broadcasted_iota(jnp.int32, (cells_y, count), 0)
    weight_x = jnp.where(x_ids == base_x, 1.0 - frac_x, 0.0) + jnp.where(x_ids == base_x + 1, frac_x, 0.0)
    weight_y = jnp.where(y_ids == base_y, 1.0 - frac_y, 0.0) + jnp.where(y_ids == base_y + 1, frac_y, 0.0)
    edge_x = jnp.where(base_x + 1 == cells_x, frac_x, 0.0)
    edge_y = jnp.where(base_y + 1 == cells_y, frac_y, 0.0)
    weight_main = weight_x[:, None, :] * weight_y[None, :, :]
    weight_extra = jnp.concatenate(
        [edge_x[None] * weight_y, weight_x * edge_y[None], (edge_x * edge_y)[None]], axis=0
    )
    values = jnp.sum(contract(main) * weight_main[None], axis=(1, 2))
    return values + jnp.sum(contract(extra) * weight_extra[None], axis=1)


def pair_sums(own_tiles, other_tiles):
    separations = [own_tiles[c][:, None, :] - other_tiles[c][:, :, None] for c in range(3)]
    distance = jnp.sqrt(sum(separation * separation for separation in separations))
    closeness = jnp.maximum(1.0 - distance, 0.0)
    weight = 20.0 * closeness * closeness * closeness * other_tiles[7][:, :, None]
    push_term = (own_tiles[6][:, None, :] + other_tiles[6][:, :, None]) * weight
    weight_total = jnp.sum(weight, axis=1)
    result = []
    for channel, separation in enumerate(separations):
        drag_term = (
            jnp.sum(weight * other_tiles[3 + channel][:, :, None], axis=1)
            - weight_total * own_tiles[3 + channel]
        )
        result.append(jnp.sum(push_term * separation, axis=1) + VISCOSITY * drag_term)
    return jnp.stack(result)


def pieces(values):
    high = lax.reduce_precision(values, exponent_bits=8, mantissa_bits=7)
    rest = values - high
    middle = lax.reduce_precision(rest, exponent_bits=8, mantissa_bits=7)
    low = rest - middle
    return jnp.concatenate([high, middle, low], axis=0).astype(jnp.bfloat16)


def joined(parts, count):
    return (parts[:count] + parts[count : 2 * count]) + parts[2 * count :]


def per_device(
    fv_state,
    buffer_owner,
    buffer_cell,
    buffer_frac,
    buffer_count,
    sph_offset,
    sph_vel,
    sph_press,
    tile_count,
):
    grid_x = lax.axis_size("gx")
    grid_y = lax.axis_size("gy")
    x_lo = from_behind(fv_state[:, -1:], "gx", 1)
    x_hi = from_behind(fv_state[:, :1], "gx", -1)
    y_lo = from_behind(fv_state[:, :, -1:], "gy", 1)
    y_hi = from_behind(fv_state[:, :, :1], "gy", -1)
    fv_next, first_row, first_column, first_corner = flux_sweep(fv_state, x_lo, x_hi, y_lo, y_hi)
    row_next = from_behind(first_row, "gx", -1)
    column_next = from_behind(first_column, "gy", -1)
    corner_next = from_diagonal(first_corner)
    extra = jnp.concatenate([row_next, column_next, corner_next[:, None]], axis=1)
    devices = grid_x * grid_y
    buffer_rows = buffer_cell.shape[0]
    capacity = 2 * buffer_rows // devices
    slot_total = devices * capacity
    owner_ids = buffer_owner[:, 0]
    row_ids = jnp.arange(buffer_rows, dtype=jnp.int32)
    is_live = row_ids < buffer_count[0]
    one_hot = (owner_ids[:, None] == jnp.arange(devices, dtype=jnp.int32)[None, :]) & is_live[
        :, None
    ]
    one_hot_float = one_hot.astype(jnp.bfloat16)
    lower_mask = (row_ids[None, :] < row_ids[:, None]).astype(jnp.bfloat16)
    earlier = jnp.dot(lower_mask, one_hot_float, preferred_element_type=jnp.float32)
    ranks = jnp.sum(jnp.where(one_hot, earlier, 0.0), axis=1).astype(jnp.int32)
    target = jnp.where(is_live, owner_ids * capacity + ranks, slot_total)
    selector = (target[:, None] == jnp.arange(slot_total, dtype=jnp.int32)[None, :]).astype(
        jnp.bfloat16
    )
    request = jnp.concatenate([buffer_frac, buffer_cell[None].astype(jnp.float32)], axis=0)
    outgoing = joined(
        jnp.dot(pieces(request), selector, preferred_element_type=jnp.float32), request.shape[0]
    )
    arrived = lax.all_to_all(outgoing, ("gx", "gy"), split_axis=1, concat_axis=1, tiled=True)
    returned = lax.all_to_all(
        answer_requests(fv_next, extra, arrived), ("gx", "gy"), split_axis=1, concat_axis=1, tiled=True
    )
    picked = joined(
        lax.dot_general(
            pieces(returned),
            selector,
            (((1,), (1,)), ((), ())),
            preferred_element_type=jnp.float32,
        ),
        returned.shape[0],
    )
    buffer_state = jnp.where(is_live[None, :], picked, 0.0)
    tiles_x, tiles_y, tile_slots = sph_press.shape
    tile_live = (
        jnp.arange(tile_slots, dtype=jnp.int32)[None, None, :] < tile_count[:, :, None]
    ).astype(jnp.float32)
    packed = jnp.concatenate([sph_offset, sph_vel, sph_press[None], tile_live[None]], axis=0)
    framed = padded_2(packed, (("gx", 1), ("gy", 2)), 1)
    own_tiles = packed.reshape(8, tiles_x * tiles_y, tile_slots)
    neighbours = []
    for corner in range(9):
        step_x = corner // 3 - 1
        step_y = corner % 3 - 1
        window = framed[:, 1 + step_x : 1 + step_x + tiles_x, 1 + step_y : 1 + step_y + tiles_y]
        shift = jnp.array([step_x, step_y, 0, 0, 0, 0, 0, 0], jnp.float32)[:, None, None, None]
        neighbours.append(window + shift)
    other_tiles = jnp.stack(neighbours, axis=3).reshape(8, tiles_x * tiles_y, 9 * tile_slots)
    total = pair_sums(own_tiles, other_tiles)
    sph_accel = (FORCE_SCALE * total * own_tiles[7][None]).reshape(3, tiles_x, tiles_y, tile_slots)
    return (fv_next, buffer_state, sph_accel)


def solution(mesh):
    return jax.shard_map(
        per_device,
        mesh=mesh,
        in_specs=(
            P(None, "gx", "gy", None),
            P(("gx", "gy"), None),
            P(("gx", "gy")),
            P(None, ("gx", "gy")),
            P(("gx", "gy")),
            P(None, "gx", "gy", None),
            P(None, "gx", "gy", None),
            P("gx", "gy", None),
            P("gx", "gy"),
        ),
        out_specs=(P(None, "gx", "gy", None), P(None, ("gx", "gy")), P(None, "gx", "gy", None)),
        check_vma=False,
    )
```

```python
import jax
import jax.numpy as jnp
from jax import lax
from jax.experimental import pallas as pl
from jax.experimental.pallas import tpu as pltpu
from jax.sharding import PartitionSpec as P

STEP_RATIO = 0.3
VISCOSITY = 0.02
FORCE_SCALE = 0.1


def padded_2(array, sides, width):
    for axis, dim in sides:
        count, length = (lax.axis_size(axis), array.shape[dim])
        up = [(i, (i + 1) % count) for i in range(count - 1)]
        down = [(j, i) for i, j in up]
        last = lax.slice_in_dim(array, length - width, length, axis=dim)
        leading = lax.slice_in_dim(array, 0, width, axis=dim)
        before = lax.ppermute(last, axis, up)
        after = lax.ppermute(leading, axis, down)
        array = jnp.concatenate([before, array, after], axis=dim)
    return array


def from_behind(array, axis, by):
    count = lax.axis_size(axis)
    pairs = [(i, i + by) for i in range(count) if 0 <= i + by < count]
    return lax.ppermute(array, axis, pairs)


def face_flux(left_side, right_side, normal):
    jump_term = right_side - left_side
    fluxes = [-0.5 * jump_term[channel] for channel in range(4)]
    fluxes[0] = fluxes[0] + 0.5 * (left_side[normal] + right_side[normal])
    fluxes[normal] = fluxes[normal] + 0.5 * (left_side[0] + right_side[0])
    return jnp.stack(fluxes)


def flux_kernel(
    state_ref, x_lo_ref, x_hi_ref, y_lo_ref, y_hi_ref, out_ref, row_ref, column_ref, corner_ref, table_ref
):
    channels, rows, cols, depth = state_ref.shape
    main_rows = channels * rows * cols
    table_ref[main_rows:, :] = jnp.zeros((table_ref.shape[0] - main_rows, depth), jnp.float32)
    col_ids = lax.broadcasted_iota(jnp.int32, (cols, depth), 0)
    lane_ids = lax.broadcasted_iota(jnp.int32, (cols, depth), 1)
    for x in range(rows):
        centre = [state_ref[c, x] for c in range(channels)]
        ahead = [state_ref[c, x + 1] if x + 1 < rows else x_hi_ref[c, 0] for c in range(channels)]
        behind = [state_ref[c, x - 1] if x > 0 else x_lo_ref[c, 0] for c in range(channels)]
        up_y = [
            jnp.where(col_ids == cols - 1, y_hi_ref[c, x], pltpu.roll(centre[c], cols - 1, 0))
            for c in range(channels)
        ]
        down_y = [
            jnp.where(col_ids == 0, y_lo_ref[c, x], pltpu.roll(centre[c], 1, 0))
            for c in range(channels)
        ]
        up_z = [
            jnp.where(lane_ids == depth - 1, 0.0, pltpu.roll(centre[c], depth - 1, 1))
            for c in range(channels)
        ]
        down_z = [jnp.where(lane_ids == 0, 0.0, pltpu.roll(centre[c], 1, 1)) for c in range(channels)]
        change = None
        for normal, (lower, upper) in ((1, (behind, ahead)), (2, (down_y, up_y)), (3, (down_z, up_z))):
            high = face_flux_list(centre, upper, normal)
            low = face_flux_list(lower, centre, normal)
            step = [high[c] - low[c] for c in range(channels)]
            change = step if change is None else [change[c] + step[c] for c in range(channels)]
        for c in range(channels):
            result = centre[c] - STEP_RATIO * change[c]
            out_ref[c, x] = result
            table_ref[(c * rows + x) * cols : (c * rows + x + 1) * cols, :] = result
            column_ref[c, x : x + 1] = result[0:1]
            if x == 0:
                row_ref[c] = result
                corner_ref[c : c + 1] = result[0:1]


def face_flux_list(left_side, right_side, normal):
    fluxes = [-0.5 * (right_side[c] - left_side[c]) for c in range(len(left_side))]
    fluxes[0] = fluxes[0] + 0.5 * (left_side[normal] + right_side[normal])
    fluxes[normal] = fluxes[normal] + 0.5 * (left_side[0] + right_side[0])
    return fluxes


def table_rows(channels, rows, cols):
    used = channels * (rows * cols + rows + cols + 1)
    return -(-used // 128) * 128


def flux_sweep(state, x_lo, x_hi, y_lo, y_hi):
    channels, rows, cols, depth = state.shape
    return pl.pallas_call(
        flux_kernel,
        out_shape=(
            jax.ShapeDtypeStruct(state.shape, state.dtype),
            jax.ShapeDtypeStruct((channels, cols, depth), state.dtype),
            jax.ShapeDtypeStruct((channels, rows, depth), state.dtype),
            jax.ShapeDtypeStruct((channels, depth), state.dtype),
            jax.ShapeDtypeStruct((table_rows(channels, rows, cols), depth), state.dtype),
        ),
    )(state, x_lo, x_hi, y_lo, y_hi)


def from_diagonal(array):
    count_x = lax.axis_size("gx")
    count_y = lax.axis_size("gy")
    pairs = [
        ((i + 1) * count_y + j + 1, i * count_y + j)
        for i in range(count_x - 1)
        for j in range(count_y - 1)
    ]
    return lax.ppermute(array, ("gx", "gy"), pairs)


def answer_requests(table, shape, arrived):
    channels, cells_x, cells_y, cells_z = shape
    count = arrived.shape[1]
    cell_index = arrived[3].astype(jnp.int32)
    base_x = cell_index // (cells_y * cells_z)
    base_y = cell_index // cells_z % cells_y
    base_z = cell_index % cells_z
    frac_x, frac_y, frac_z = arrived[0], arrived[1], arrived[2]
    z_ids = lax.broadcasted_iota(jnp.int32, (cells_z, count), 0)
    z_weight = jnp.where(z_ids == base_z[None, :], 1.0 - frac_z[None, :], 0.0) + jnp.where(
        z_ids == base_z[None, :] + 1, frac_z[None, :], 0.0
    )
    columns = lax.dot_general(
        table,
        z_weight,
        (((1,), (0,)), ((), ())),
        precision=lax.Precision.HIGH,
        preferred_element_type=jnp.float32,
    )
    x_ids = lax.broadcasted_iota(jnp.int32, (cells_x, count), 0)
    y_ids = lax.broadcasted_iota(jnp.int32, (cells_y, count), 0)
    weight_x = jnp.where(x_ids == base_x, 1.0 - frac_x, 0.0) + jnp.where(x_ids == base_x + 1, frac_x, 0.0)
    weight_y = jnp.where(y_ids == base_y, 1.0 - frac_y, 0.0) + jnp.where(y_ids == base_y + 1, frac_y, 0.0)
    edge_x = jnp.where(base_x + 1 == cells_x, frac_x, 0.0)
    edge_y = jnp.where(base_y + 1 == cells_y, frac_y, 0.0)
    weight_main = (weight_x[:, None, :] * weight_y[None, :, :]).reshape(cells_x * cells_y, count)
    weight_extra = jnp.concatenate(
        [edge_x[None] * weight_y, weight_x * edge_y[None], (edge_x * edge_y)[None]], axis=0
    )
    main_rows = cells_x * cells_y
    extra_rows = cells_x + cells_y + 1
    values = []
    for c in range(channels):
        main = columns[c * main_rows : (c + 1) * main_rows]
        start = channels * main_rows + c * extra_rows
        extra = columns[start : start + extra_rows]
        values.append(jnp.sum(main * weight_main, axis=0) + jnp.sum(extra * weight_extra, axis=0))
    return jnp.stack(values)


def pair_sums(own_tiles, other_tiles):
    separations = [own_tiles[c][:, None, :] - other_tiles[c][:, :, None] for c in range(3)]
    distance = jnp.sqrt(sum(separation * separation for separation in separations))
    closeness = jnp.maximum(1.0 - distance, 0.0)
    weight = 20.0 * closeness * closeness * closeness * other_tiles[7][:, :, None]
    push_term = (own_tiles[6][:, None, :] + other_tiles[6][:, :, None]) * weight
    weight_total = jnp.sum(weight, axis=1)
    result = []
    for channel, separation in enumerate(separations):
        drag_term = (
            jnp.sum(weight * other_tiles[3 + channel][:, :, None], axis=1)
            - weight_total * own_tiles[3 + channel]
        )
        result.append(jnp.sum(push_term * separation, axis=1) + VISCOSITY * drag_term)
    return jnp.stack(result)


def pieces(values):
    high = lax.reduce_precision(values, exponent_bits=8, mantissa_bits=7)
    rest = values - high
    middle = lax.reduce_precision(rest, exponent_bits=8, mantissa_bits=7)
    low = rest - middle
    return jnp.concatenate([high, middle, low], axis=0).astype(jnp.bfloat16)


def joined(parts, count):
    return (parts[:count] + parts[count : 2 * count]) + parts[2 * count :]


def per_device(
    fv_state,
    buffer_owner,
    buffer_cell,
    buffer_frac,
    buffer_count,
    sph_offset,
    sph_vel,
    sph_press,
    tile_count,
):
    grid_x = lax.axis_size("gx")
    grid_y = lax.axis_size("gy")
    x_lo = from_behind(fv_state[:, -1:], "gx", 1)
    x_hi = from_behind(fv_state[:, :1], "gx", -1)
    y_lo = from_behind(fv_state[:, :, -1:], "gy", 1)
    y_hi = from_behind(fv_state[:, :, :1], "gy", -1)
    fv_next, first_row, first_column, first_corner, table = flux_sweep(
        fv_state, x_lo, x_hi, y_lo, y_hi
    )
    row_next = from_behind(first_row, "gx", -1)
    column_next = from_behind(first_column, "gy", -1)
    corner_next = from_diagonal(first_corner)
    extra = jnp.concatenate([row_next, column_next, corner_next[:, None]], axis=1)
    table = lax.dynamic_update_slice(
        table, extra.reshape(-1, extra.shape[-1]), (fv_next.size // fv_next.shape[-1], 0)
    )
    devices = grid_x * grid_y
    buffer_rows = buffer_cell.shape[0]
    capacity = 2 * buffer_rows // devices
    slot_total = devices * capacity
    owner_ids = buffer_owner[:, 0]
    row_ids = jnp.arange(buffer_rows, dtype=jnp.int32)
    is_live = row_ids < buffer_count[0]
    one_hot = (owner_ids[:, None] == jnp.arange(devices, dtype=jnp.int32)[None, :]) & is_live[
        :, None
    ]
    one_hot_float = one_hot.astype(jnp.bfloat16)
    lower_mask = (row_ids[None, :] < row_ids[:, None]).astype(jnp.bfloat16)
    earlier = jnp.dot(lower_mask, one_hot_float, preferred_element_type=jnp.float32)
    ranks = jnp.sum(jnp.where(one_hot, earlier, 0.0), axis=1).astype(jnp.int32)
    target = jnp.where(is_live, owner_ids * capacity + ranks, slot_total)
    selector = (target[:, None] == jnp.arange(slot_total, dtype=jnp.int32)[None, :]).astype(
        jnp.bfloat16
    )
    request = jnp.concatenate([buffer_frac, buffer_cell[None].astype(jnp.float32)], axis=0)
    outgoing = joined(
        jnp.dot(pieces(request), selector, preferred_element_type=jnp.float32), request.shape[0]
    )
    arrived = lax.all_to_all(outgoing, ("gx", "gy"), split_axis=1, concat_axis=1, tiled=True)
    returned = lax.all_to_all(
        answer_requests(table, fv_next.shape, arrived), ("gx", "gy"), split_axis=1, concat_axis=1, tiled=True
    )
    picked = joined(
        lax.dot_general(
            pieces(returned),
            selector,
            (((1,), (1,)), ((), ())),
            preferred_element_type=jnp.float32,
        ),
        returned.shape[0],
    )
    buffer_state = jnp.where(is_live[None, :], picked, 0.0)
    tiles_x, tiles_y, tile_slots = sph_press.shape
    tile_live = (
        jnp.arange(tile_slots, dtype=jnp.int32)[None, None, :] < tile_count[:, :, None]
    ).astype(jnp.float32)
    packed = jnp.concatenate([sph_offset, sph_vel, sph_press[None], tile_live[None]], axis=0)
    framed = padded_2(packed, (("gx", 1), ("gy", 2)), 1)
    own_tiles = packed.reshape(8, tiles_x * tiles_y, tile_slots)
    neighbours = []
    for corner in range(9):
        step_x = corner // 3 - 1
        step_y = corner % 3 - 1
        window = framed[:, 1 + step_x : 1 + step_x + tiles_x, 1 + step_y : 1 + step_y + tiles_y]
        shift = jnp.array([step_x, step_y, 0, 0, 0, 0, 0, 0], jnp.float32)[:, None, None, None]
        neighbours.append(window + shift)
    other_tiles = jnp.stack(neighbours, axis=3).reshape(8, tiles_x * tiles_y, 9 * tile_slots)
    total = pair_sums(own_tiles, other_tiles)
    sph_accel = (FORCE_SCALE * total * own_tiles[7][None]).reshape(3, tiles_x, tiles_y, tile_slots)
    return (fv_next, buffer_state, sph_accel)


def solution(mesh):
    return jax.shard_map(
        per_device,
        mesh=mesh,
        in_specs=(
            P(None, "gx", "gy", None),
            P(("gx", "gy"), None),
            P(("gx", "gy")),
            P(None, ("gx", "gy")),
            P(("gx", "gy")),
            P(None, "gx", "gy", None),
            P(None, "gx", "gy", None),
            P("gx", "gy", None),
            P("gx", "gy"),
        ),
        out_specs=(P(None, "gx", "gy", None), P(None, ("gx", "gy")), P(None, "gx", "gy", None)),
        check_vma=False,
    )
```

```python
import jax
import jax.numpy as jnp
from jax import lax
from jax.experimental import pallas as pl
from jax.experimental.pallas import tpu as pltpu
from jax.sharding import PartitionSpec as P


STEP_RATIO = 0.3
VISCOSITY = 0.02
FORCE_SCALE = 0.1


def padded_2(array, sides, width):
    for axis, dim in sides:
        count, length = (lax.axis_size(axis), array.shape[dim])
        up = [(i, (i + 1) % count) for i in range(count - 1)]
        down = [(j, i) for i, j in up]
        last = lax.slice_in_dim(array, length - width, length, axis=dim)
        leading = lax.slice_in_dim(array, 0, width, axis=dim)
        before = lax.ppermute(last, axis, up)
        after = lax.ppermute(leading, axis, down)
        array = jnp.concatenate([before, array, after], axis=dim)
    return array


def from_behind(array, axis, by):
    count = lax.axis_size(axis)
    pairs = [(i, i + by) for i in range(count) if 0 <= i + by < count]
    return lax.ppermute(array, axis, pairs)


def flux_kernel(
    state_ref, x_lo_ref, x_hi_ref, y_lo_ref, y_hi_ref, out_ref, row_ref, column_ref, corner_ref, table_ref
):
    channels, rows, cols, depth = state_ref.shape
    main_rows = channels * rows * cols
    table_ref[main_rows:, :] = jnp.zeros((table_ref.shape[0] - main_rows, depth), jnp.float32)
    col_ids = lax.broadcasted_iota(jnp.int32, (cols, depth), 0)
    lane_ids = lax.broadcasted_iota(jnp.int32, (cols, depth), 1)
    for x in range(rows):
        centre = [state_ref[c, x] for c in range(channels)]
        ahead = [state_ref[c, x + 1] if x + 1 < rows else x_hi_ref[c, 0] for c in range(channels)]
        behind = [state_ref[c, x - 1] if x > 0 else x_lo_ref[c, 0] for c in range(channels)]
        up_y = [
            jnp.where(col_ids == cols - 1, y_hi_ref[c, x], pltpu.roll(centre[c], cols - 1, 0))
            for c in range(channels)
        ]
        down_y = [
            jnp.where(col_ids == 0, y_lo_ref[c, x], pltpu.roll(centre[c], 1, 0))
            for c in range(channels)
        ]
        up_z = [
            jnp.where(lane_ids == depth - 1, 0.0, pltpu.roll(centre[c], depth - 1, 1))
            for c in range(channels)
        ]
        down_z = [jnp.where(lane_ids == 0, 0.0, pltpu.roll(centre[c], 1, 1)) for c in range(channels)]
        change = None
        for normal, (lower, upper) in ((1, (behind, ahead)), (2, (down_y, up_y)), (3, (down_z, up_z))):
            high = face_flux_list(centre, upper, normal)
            low = face_flux_list(lower, centre, normal)
            step = [high[c] - low[c] for c in range(channels)]
            change = step if change is None else [change[c] + step[c] for c in range(channels)]
        for c in range(channels):
            result = centre[c] - STEP_RATIO * change[c]
            out_ref[c, x] = result
            table_ref[(c * rows + x) * cols : (c * rows + x + 1) * cols, :] = result
            column_ref[c, x : x + 1] = result[0:1]
            if x == 0:
                row_ref[c] = result
                corner_ref[c : c + 1] = result[0:1]


def face_flux_list(left_side, right_side, normal):
    fluxes = [-0.5 * (right_side[c] - left_side[c]) for c in range(len(left_side))]
    fluxes[0] = fluxes[0] + 0.5 * (left_side[normal] + right_side[normal])
    fluxes[normal] = fluxes[normal] + 0.5 * (left_side[0] + right_side[0])
    return fluxes


def table_rows(channels, rows, cols):
    used = channels * (rows * cols + rows + cols + 1)
    return -(-used // 128) * 128


def flux_sweep(state, x_lo, x_hi, y_lo, y_hi):
    channels, rows, cols, depth = state.shape
    return pl.pallas_call(
        flux_kernel,
        out_shape=(
            jax.ShapeDtypeStruct(state.shape, state.dtype),
            jax.ShapeDtypeStruct((channels, cols, depth), state.dtype),
            jax.ShapeDtypeStruct((channels, rows, depth), state.dtype),
            jax.ShapeDtypeStruct((channels, depth), state.dtype),
            jax.ShapeDtypeStruct((table_rows(channels, rows, cols), depth), state.dtype),
        ),
    )(state, x_lo, x_hi, y_lo, y_hi)


def from_diagonal(array):
    count_x = lax.axis_size("gx")
    count_y = lax.axis_size("gy")
    pairs = [
        ((i + 1) * count_y + j + 1, i * count_y + j)
        for i in range(count_x - 1)
        for j in range(count_y - 1)
    ]
    return lax.ppermute(array, ("gx", "gy"), pairs)


def answer_requests(table, shape, arrived):
    channels, cells_x, cells_y, cells_z = shape
    count = arrived.shape[1]
    cell_index = arrived[3].astype(jnp.int32)
    base_x = cell_index // (cells_y * cells_z)
    base_y = cell_index // cells_z % cells_y
    base_z = cell_index % cells_z
    frac_x, frac_y, frac_z = arrived[0], arrived[1], arrived[2]
    z_ids = lax.broadcasted_iota(jnp.int32, (cells_z, count), 0)
    z_weight = jnp.where(z_ids == base_z[None, :], 1.0 - frac_z[None, :], 0.0) + jnp.where(
        z_ids == base_z[None, :] + 1, frac_z[None, :], 0.0
    )
    columns = lax.dot_general(
        table,
        z_weight,
        (((1,), (0,)), ((), ())),
        precision=lax.Precision.HIGH,
        preferred_element_type=jnp.float32,
    )
    x_ids = lax.broadcasted_iota(jnp.int32, (cells_x, count), 0)
    y_ids = lax.broadcasted_iota(jnp.int32, (cells_y, count), 0)
    weight_x = jnp.where(x_ids == base_x, 1.0 - frac_x, 0.0) + jnp.where(x_ids == base_x + 1, frac_x, 0.0)
    weight_y = jnp.where(y_ids == base_y, 1.0 - frac_y, 0.0) + jnp.where(y_ids == base_y + 1, frac_y, 0.0)
    edge_x = jnp.where(base_x + 1 == cells_x, frac_x, 0.0)
    edge_y = jnp.where(base_y + 1 == cells_y, frac_y, 0.0)
    weight_main = (weight_x[:, None, :] * weight_y[None, :, :]).reshape(cells_x * cells_y, count)
    weight_extra = jnp.concatenate(
        [edge_x[None] * weight_y, weight_x * edge_y[None], (edge_x * edge_y)[None]], axis=0
    )
    main_rows = cells_x * cells_y
    extra_rows = cells_x + cells_y + 1
    values = []
    for c in range(channels):
        main = columns[c * main_rows : (c + 1) * main_rows]
        start = channels * main_rows + c * extra_rows
        extra = columns[start : start + extra_rows]
        values.append(jnp.sum(main * weight_main, axis=0) + jnp.sum(extra * weight_extra, axis=0))
    return jnp.stack(values)


def pair_sums(own_tiles, other_tiles):
    separations = [own_tiles[c][:, None, :] - other_tiles[c][:, :, None] for c in range(3)]
    distance = jnp.sqrt(sum(separation * separation for separation in separations))
    closeness = jnp.maximum(1.0 - distance, 0.0)
    weight = 20.0 * closeness * closeness * closeness * other_tiles[7][:, :, None]
    push_term = (own_tiles[6][:, None, :] + other_tiles[6][:, :, None]) * weight
    weight_total = jnp.sum(weight, axis=1)
    result = []
    for channel, separation in enumerate(separations):
        drag_term = (
            jnp.sum(weight * other_tiles[3 + channel][:, :, None], axis=1)
            - weight_total * own_tiles[3 + channel]
        )
        result.append(jnp.sum(push_term * separation, axis=1) + VISCOSITY * drag_term)
    return jnp.stack(result)


def pieces(values):
    high = lax.reduce_precision(values, exponent_bits=8, mantissa_bits=7)
    rest = values - high
    middle = lax.reduce_precision(rest, exponent_bits=8, mantissa_bits=7)
    low = rest - middle
    return jnp.concatenate([high, middle, low], axis=0).astype(jnp.bfloat16)


def joined(parts, count):
    return (parts[:count] + parts[count : 2 * count]) + parts[2 * count :]


def step_body(
    fv_state,
    buffer_owner,
    buffer_cell,
    buffer_frac,
    buffer_count,
    sph_offset,
    sph_vel,
    sph_press,
    tile_count,
):
    grid_x = lax.axis_size("gx")
    grid_y = lax.axis_size("gy")
    devices = grid_x * grid_y
    buffer_rows = buffer_cell.shape[0]
    capacity = 2 * buffer_rows // devices
    slot_total = devices * capacity
    owner_ids = buffer_owner[:, 0]
    row_ids = jnp.arange(buffer_rows, dtype=jnp.int32)
    is_live = row_ids < buffer_count[0]
    one_hot = (owner_ids[:, None] == jnp.arange(devices, dtype=jnp.int32)[None, :]) & is_live[
        :, None
    ]
    one_hot_float = one_hot.astype(jnp.bfloat16)
    lower_mask = (row_ids[None, :] < row_ids[:, None]).astype(jnp.bfloat16)
    earlier = jnp.dot(lower_mask, one_hot_float, preferred_element_type=jnp.float32)
    ranks = jnp.sum(jnp.where(one_hot, earlier, 0.0), axis=1).astype(jnp.int32)
    target = jnp.where(is_live, owner_ids * capacity + ranks, slot_total)
    selector = (target[:, None] == jnp.arange(slot_total, dtype=jnp.int32)[None, :]).astype(
        jnp.bfloat16
    )
    request = jnp.concatenate([buffer_frac, buffer_cell[None].astype(jnp.float32)], axis=0)
    outgoing = joined(
        jnp.dot(pieces(request), selector, preferred_element_type=jnp.float32), request.shape[0]
    )
    arrived = lax.all_to_all(outgoing, ("gx", "gy"), split_axis=1, concat_axis=1, tiled=True)
    fv_state, arrived = lax.optimization_barrier((fv_state, arrived))
    x_lo = from_behind(fv_state[:, -1:], "gx", 1)
    x_hi = from_behind(fv_state[:, :1], "gx", -1)
    y_lo = from_behind(fv_state[:, :, -1:], "gy", 1)
    y_hi = from_behind(fv_state[:, :, :1], "gy", -1)
    fv_next, first_row, first_column, first_corner, table = flux_sweep(
        fv_state, x_lo, x_hi, y_lo, y_hi
    )
    row_next = from_behind(first_row, "gx", -1)
    column_next = from_behind(first_column, "gy", -1)
    corner_next = from_diagonal(first_corner)
    extra = jnp.concatenate([row_next, column_next, corner_next[:, None]], axis=1)
    table = lax.dynamic_update_slice(
        table, extra.reshape(-1, extra.shape[-1]), (fv_next.size // fv_next.shape[-1], 0)
    )
    returned = lax.all_to_all(
        answer_requests(table, fv_next.shape, arrived), ("gx", "gy"), split_axis=1, concat_axis=1, tiled=True
    )
    picked = joined(
        lax.dot_general(
            pieces(returned),
            selector,
            (((1,), (1,)), ((), ())),
            preferred_element_type=jnp.float32,
        ),
        returned.shape[0],
    )
    buffer_state = jnp.where(is_live[None, :], picked, 0.0)
    tiles_x, tiles_y, tile_slots = sph_press.shape
    tile_live = (
        jnp.arange(tile_slots, dtype=jnp.int32)[None, None, :] < tile_count[:, :, None]
    ).astype(jnp.float32)
    packed = jnp.concatenate([sph_offset, sph_vel, sph_press[None], tile_live[None]], axis=0)
    framed = padded_2(packed, (("gx", 1), ("gy", 2)), 1)
    own_tiles = packed.reshape(8, tiles_x * tiles_y, tile_slots)
    neighbours = []
    for corner in range(9):
        step_x = corner // 3 - 1
        step_y = corner % 3 - 1
        window = framed[:, 1 + step_x : 1 + step_x + tiles_x, 1 + step_y : 1 + step_y + tiles_y]
        shift = jnp.array([step_x, step_y, 0, 0, 0, 0, 0, 0], jnp.float32)[:, None, None, None]
        neighbours.append(window + shift)
    other_tiles = jnp.stack(neighbours, axis=3).reshape(8, tiles_x * tiles_y, 9 * tile_slots)
    total = pair_sums(own_tiles, other_tiles)
    sph_accel = (FORCE_SCALE * total * own_tiles[7][None]).reshape(3, tiles_x, tiles_y, tile_slots)
    return (fv_next, buffer_state, sph_accel)


def solution(mesh):
    return sharded(mesh)


def sharded(mesh):
    return jax.shard_map(
        step_body,
        mesh=mesh,
        in_specs=(
            P(None, "gx", "gy", None),
            P(("gx", "gy"), None),
            P(("gx", "gy")),
            P(None, ("gx", "gy")),
            P(("gx", "gy")),
            P(None, "gx", "gy", None),
            P(None, "gx", "gy", None),
            P("gx", "gy", None),
            P("gx", "gy"),
        ),
        out_specs=(P(None, "gx", "gy", None), P(None, ("gx", "gy")), P(None, "gx", "gy", None)),
        check_vma=False,
    )
```

```python
import jax
import jax.numpy as jnp
from jax import lax
from jax.experimental import pallas as pl
from jax.experimental.pallas import tpu as pltpu
from jax.sharding import PartitionSpec as P


STEP_RATIO = 0.3
VISCOSITY = 0.02
FORCE_SCALE = 0.1


def padded_2(array, sides, width):
    for axis, dim in sides:
        count, length = (lax.axis_size(axis), array.shape[dim])
        up = [(i, (i + 1) % count) for i in range(count - 1)]
        down = [(j, i) for i, j in up]
        last = lax.slice_in_dim(array, length - width, length, axis=dim)
        leading = lax.slice_in_dim(array, 0, width, axis=dim)
        before = lax.ppermute(last, axis, up)
        after = lax.ppermute(leading, axis, down)
        array = jnp.concatenate([before, array, after], axis=dim)
    return array


def from_behind(array, axis, by):
    count = lax.axis_size(axis)
    pairs = [(i, i + by) for i in range(count) if 0 <= i + by < count]
    return lax.ppermute(array, axis, pairs)


def flux_kernel(
    state_ref, x_lo_ref, x_hi_ref, y_lo_ref, y_hi_ref, out_ref, row_ref, column_ref, corner_ref, table_ref
):
    channels, rows, cols, depth = state_ref.shape
    main_rows = channels * rows * cols
    table_ref[main_rows:, :] = jnp.zeros((table_ref.shape[0] - main_rows, depth), jnp.float32)
    col_ids = lax.broadcasted_iota(jnp.int32, (cols, depth), 0)
    lane_ids = lax.broadcasted_iota(jnp.int32, (cols, depth), 1)
    for x in range(rows):
        centre = [state_ref[c, x] for c in range(channels)]
        ahead = [state_ref[c, x + 1] if x + 1 < rows else x_hi_ref[c, 0] for c in range(channels)]
        behind = [state_ref[c, x - 1] if x > 0 else x_lo_ref[c, 0] for c in range(channels)]
        up_y = [
            jnp.where(col_ids == cols - 1, y_hi_ref[c, x], pltpu.roll(centre[c], cols - 1, 0))
            for c in range(channels)
        ]
        down_y = [
            jnp.where(col_ids == 0, y_lo_ref[c, x], pltpu.roll(centre[c], 1, 0))
            for c in range(channels)
        ]
        up_z = [
            jnp.where(lane_ids == depth - 1, 0.0, pltpu.roll(centre[c], depth - 1, 1))
            for c in range(channels)
        ]
        down_z = [jnp.where(lane_ids == 0, 0.0, pltpu.roll(centre[c], 1, 1)) for c in range(channels)]
        change = None
        for normal, (lower, upper) in ((1, (behind, ahead)), (2, (down_y, up_y)), (3, (down_z, up_z))):
            high = face_flux_list(centre, upper, normal)
            low = face_flux_list(lower, centre, normal)
            step = [high[c] - low[c] for c in range(channels)]
            change = step if change is None else [change[c] + step[c] for c in range(channels)]
        for c in range(channels):
            result = centre[c] - STEP_RATIO * change[c]
            out_ref[c, x] = result
            table_ref[(c * rows + x) * cols : (c * rows + x + 1) * cols, :] = result
            column_ref[c, x : x + 1] = result[0:1]
            if x == 0:
                row_ref[c] = result
                corner_ref[c : c + 1] = result[0:1]


def face_flux_list(left_side, right_side, normal):
    fluxes = [-0.5 * (right_side[c] - left_side[c]) for c in range(len(left_side))]
    fluxes[0] = fluxes[0] + 0.5 * (left_side[normal] + right_side[normal])
    fluxes[normal] = fluxes[normal] + 0.5 * (left_side[0] + right_side[0])
    return fluxes


def table_rows(channels, rows, cols):
    used = channels * (rows * cols + rows + cols + 1)
    return -(-used // 128) * 128


def flux_sweep(state, x_lo, x_hi, y_lo, y_hi):
    channels, rows, cols, depth = state.shape
    return pl.pallas_call(
        flux_kernel,
        out_shape=(
            jax.ShapeDtypeStruct(state.shape, state.dtype),
            jax.ShapeDtypeStruct((channels, cols, depth), state.dtype),
            jax.ShapeDtypeStruct((channels, rows, depth), state.dtype),
            jax.ShapeDtypeStruct((channels, depth), state.dtype),
            jax.ShapeDtypeStruct((table_rows(channels, rows, cols), depth), state.dtype),
        ),
    )(state, x_lo, x_hi, y_lo, y_hi)


def from_diagonal(array):
    count_x = lax.axis_size("gx")
    count_y = lax.axis_size("gy")
    pairs = [
        ((i + 1) * count_y + j + 1, i * count_y + j)
        for i in range(count_x - 1)
        for j in range(count_y - 1)
    ]
    return lax.ppermute(array, ("gx", "gy"), pairs)


def answer_requests(table, shape, arrived):
    channels, cells_x, cells_y, cells_z = shape
    count = arrived.shape[1]
    cell_index = arrived[3].astype(jnp.int32)
    base_x = cell_index // (cells_y * cells_z)
    base_y = cell_index // cells_z % cells_y
    base_z = cell_index % cells_z
    frac_x, frac_y, frac_z = arrived[0], arrived[1], arrived[2]
    z_ids = lax.broadcasted_iota(jnp.int32, (cells_z, count), 0)
    z_weight = jnp.where(z_ids == base_z[None, :], 1.0 - frac_z[None, :], 0.0) + jnp.where(
        z_ids == base_z[None, :] + 1, frac_z[None, :], 0.0
    )
    columns = lax.dot_general(
        table,
        z_weight,
        (((1,), (0,)), ((), ())),
        precision=lax.Precision.HIGH,
        preferred_element_type=jnp.float32,
    )
    x_ids = lax.broadcasted_iota(jnp.int32, (cells_x, count), 0)
    y_ids = lax.broadcasted_iota(jnp.int32, (cells_y, count), 0)
    weight_x = jnp.where(x_ids == base_x, 1.0 - frac_x, 0.0) + jnp.where(x_ids == base_x + 1, frac_x, 0.0)
    weight_y = jnp.where(y_ids == base_y, 1.0 - frac_y, 0.0) + jnp.where(y_ids == base_y + 1, frac_y, 0.0)
    edge_x = jnp.where(base_x + 1 == cells_x, frac_x, 0.0)
    edge_y = jnp.where(base_y + 1 == cells_y, frac_y, 0.0)
    weight_main = (weight_x[:, None, :] * weight_y[None, :, :]).reshape(cells_x * cells_y, count)
    weight_extra = jnp.concatenate(
        [edge_x[None] * weight_y, weight_x * edge_y[None], (edge_x * edge_y)[None]], axis=0
    )
    main_rows = cells_x * cells_y
    extra_rows = cells_x + cells_y + 1
    values = []
    for c in range(channels):
        main = columns[c * main_rows : (c + 1) * main_rows]
        start = channels * main_rows + c * extra_rows
        extra = columns[start : start + extra_rows]
        values.append(jnp.sum(main * weight_main, axis=0) + jnp.sum(extra * weight_extra, axis=0))
    return jnp.stack(values)


def pair_sums(own_tiles, other_tiles):
    separations = [own_tiles[c][:, None, :] - other_tiles[c][:, :, None] for c in range(3)]
    distance = jnp.sqrt(sum(separation * separation for separation in separations))
    closeness = jnp.maximum(1.0 - distance, 0.0)
    weight = 20.0 * closeness * closeness * closeness * other_tiles[7][:, :, None]
    push_term = (own_tiles[6][:, None, :] + other_tiles[6][:, :, None]) * weight
    weight_total = jnp.sum(weight, axis=1)
    result = []
    for channel, separation in enumerate(separations):
        drag_term = (
            jnp.sum(weight * other_tiles[3 + channel][:, :, None], axis=1)
            - weight_total * own_tiles[3 + channel]
        )
        result.append(jnp.sum(push_term * separation, axis=1) + VISCOSITY * drag_term)
    return jnp.stack(result)


def pieces(values):
    high = lax.reduce_precision(values, exponent_bits=8, mantissa_bits=7)
    rest = values - high
    middle = lax.reduce_precision(rest, exponent_bits=8, mantissa_bits=7)
    low = rest - middle
    return jnp.concatenate([high, middle, low], axis=0).astype(jnp.bfloat16)


def joined(parts, count):
    return (parts[:count] + parts[count : 2 * count]) + parts[2 * count :]


def step_body(
    fv_state,
    buffer_owner,
    buffer_cell,
    buffer_frac,
    buffer_count,
    sph_offset,
    sph_vel,
    sph_press,
    tile_count,
):
    grid_x = lax.axis_size("gx")
    grid_y = lax.axis_size("gy")
    devices = grid_x * grid_y
    buffer_rows = buffer_cell.shape[0]
    capacity = 2 * buffer_rows // devices
    slot_total = devices * capacity
    owner_ids = buffer_owner[:, 0]
    row_ids = jnp.arange(buffer_rows, dtype=jnp.int32)
    is_live = row_ids < buffer_count[0]
    one_hot = (owner_ids[:, None] == jnp.arange(devices, dtype=jnp.int32)[None, :]) & is_live[
        :, None
    ]
    one_hot_float = one_hot.astype(jnp.bfloat16)
    lower_mask = (row_ids[None, :] < row_ids[:, None]).astype(jnp.bfloat16)
    earlier = jnp.dot(lower_mask, one_hot_float, preferred_element_type=jnp.float32)
    ranks = jnp.sum(jnp.where(one_hot, earlier, 0.0), axis=1).astype(jnp.int32)
    target = jnp.where(is_live, owner_ids * capacity + ranks, slot_total)
    selector = (target[:, None] == jnp.arange(slot_total, dtype=jnp.int32)[None, :]).astype(
        jnp.bfloat16
    )
    request = jnp.concatenate([buffer_frac, buffer_cell[None].astype(jnp.float32)], axis=0)
    outgoing = joined(
        jnp.dot(pieces(request), selector, preferred_element_type=jnp.float32), request.shape[0]
    )
    arrived = lax.all_to_all(outgoing, ("gx", "gy"), split_axis=1, concat_axis=1, tiled=True)
    fv_state, arrived = lax.optimization_barrier((fv_state, arrived))
    x_lo = from_behind(fv_state[:, -1:], "gx", 1)
    x_hi = from_behind(fv_state[:, :1], "gx", -1)
    y_lo = from_behind(fv_state[:, :, -1:], "gy", 1)
    y_hi = from_behind(fv_state[:, :, :1], "gy", -1)
    fv_next, first_row, first_column, first_corner, table = flux_sweep(
        fv_state, x_lo, x_hi, y_lo, y_hi
    )
    row_next = from_behind(first_row, "gx", -1)
    column_next = from_behind(first_column, "gy", -1)
    corner_next = from_diagonal(first_corner)
    extra = jnp.concatenate([row_next, column_next, corner_next[:, None]], axis=1)
    table = lax.dynamic_update_slice(
        table, extra.reshape(-1, extra.shape[-1]), (fv_next.size // fv_next.shape[-1], 0)
    )
    returned = lax.all_to_all(
        answer_requests(table, fv_next.shape, arrived), ("gx", "gy"), split_axis=1, concat_axis=1, tiled=True
    )
    picked = joined(
        lax.dot_general(
            pieces(returned),
            selector,
            (((1,), (1,)), ((), ())),
            preferred_element_type=jnp.float32,
        ),
        returned.shape[0],
    )
    buffer_state = jnp.where(is_live[None, :], picked, 0.0)
    tiles_x, tiles_y, tile_slots = sph_press.shape
    tile_live = (
        jnp.arange(tile_slots, dtype=jnp.int32)[None, None, :] < tile_count[:, :, None]
    ).astype(jnp.float32)
    packed = jnp.concatenate([sph_offset, sph_vel, sph_press[None], tile_live[None]], axis=0)
    framed = padded_2(packed, (("gx", 1), ("gy", 2)), 1)
    own_tiles = packed.reshape(8, tiles_x * tiles_y, tile_slots)
    neighbours = []
    for corner in range(9):
        step_x = corner // 3 - 1
        step_y = corner % 3 - 1
        window = framed[:, 1 + step_x : 1 + step_x + tiles_x, 1 + step_y : 1 + step_y + tiles_y]
        shift = jnp.array([step_x, step_y, 0, 0, 0, 0, 0, 0], jnp.float32)[:, None, None, None]
        neighbours.append(window + shift)
    other_tiles = jnp.stack(neighbours, axis=3).reshape(8, tiles_x * tiles_y, 9 * tile_slots)
    half = own_tiles.shape[1] // 2
    first_total = pair_sums(own_tiles[:, :half], other_tiles[:, :half])
    second_total = pair_sums(own_tiles[:, half:], other_tiles[:, half:])
    total = jnp.concatenate([first_total, second_total], axis=1)
    sph_accel = (FORCE_SCALE * total * own_tiles[7][None]).reshape(3, tiles_x, tiles_y, tile_slots)
    return (fv_next, buffer_state, sph_accel)


def solution(mesh):
    return sharded(mesh)


def sharded(mesh):
    return jax.shard_map(
        step_body,
        mesh=mesh,
        in_specs=(
            P(None, "gx", "gy", None),
            P(("gx", "gy"), None),
            P(("gx", "gy")),
            P(None, ("gx", "gy")),
            P(("gx", "gy")),
            P(None, "gx", "gy", None),
            P(None, "gx", "gy", None),
            P("gx", "gy", None),
            P("gx", "gy"),
        ),
        out_specs=(P(None, "gx", "gy", None), P(None, ("gx", "gy")), P(None, "gx", "gy", None)),
        check_vma=False,
    )
```

```python
import jax
import jax.numpy as jnp
from jax import lax
from jax.experimental import pallas as pl
from jax.experimental.pallas import tpu as pltpu
from jax.sharding import PartitionSpec as P


STEP_RATIO = 0.3
VISCOSITY = 0.02
FORCE_SCALE = 0.1


def from_behind(array, axis, by):
    count = lax.axis_size(axis)
    pairs = [(i, i + by) for i in range(count) if 0 <= i + by < count]
    return lax.ppermute(array, axis, pairs)


def flux_kernel(
    state_ref, x_lo_ref, x_hi_ref, y_lo_ref, y_hi_ref, out_ref, row_ref, column_ref, corner_ref, table_ref
):
    channels, rows, cols, depth = state_ref.shape
    main_rows = channels * rows * cols
    table_ref[main_rows:, :] = jnp.zeros((table_ref.shape[0] - main_rows, depth), jnp.float32)
    col_ids = lax.broadcasted_iota(jnp.int32, (cols, depth), 0)
    lane_ids = lax.broadcasted_iota(jnp.int32, (cols, depth), 1)
    for x in range(rows):
        centre = [state_ref[c, x] for c in range(channels)]
        ahead = [state_ref[c, x + 1] if x + 1 < rows else x_hi_ref[c, 0] for c in range(channels)]
        behind = [state_ref[c, x - 1] if x > 0 else x_lo_ref[c, 0] for c in range(channels)]
        up_y = [
            jnp.where(col_ids == cols - 1, y_hi_ref[c, x], pltpu.roll(centre[c], cols - 1, 0))
            for c in range(channels)
        ]
        down_y = [
            jnp.where(col_ids == 0, y_lo_ref[c, x], pltpu.roll(centre[c], 1, 0))
            for c in range(channels)
        ]
        up_z = [
            jnp.where(lane_ids == depth - 1, 0.0, pltpu.roll(centre[c], depth - 1, 1))
            for c in range(channels)
        ]
        down_z = [jnp.where(lane_ids == 0, 0.0, pltpu.roll(centre[c], 1, 1)) for c in range(channels)]
        change = None
        for normal, (lower, upper) in ((1, (behind, ahead)), (2, (down_y, up_y)), (3, (down_z, up_z))):
            high = face_flux_list(centre, upper, normal)
            low = face_flux_list(lower, centre, normal)
            step = [high[c] - low[c] for c in range(channels)]
            change = step if change is None else [change[c] + step[c] for c in range(channels)]
        for c in range(channels):
            result = centre[c] - STEP_RATIO * change[c]
            out_ref[c, x] = result
            table_ref[(c * rows + x) * cols : (c * rows + x + 1) * cols, :] = result
            column_ref[c, x : x + 1] = result[0:1]
            if x == 0:
                row_ref[c] = result
                corner_ref[c : c + 1] = result[0:1]


def face_flux_list(left_side, right_side, normal):
    fluxes = [-0.5 * (right_side[c] - left_side[c]) for c in range(len(left_side))]
    fluxes[0] = fluxes[0] + 0.5 * (left_side[normal] + right_side[normal])
    fluxes[normal] = fluxes[normal] + 0.5 * (left_side[0] + right_side[0])
    return fluxes


def table_rows(channels, rows, cols):
    used = channels * (rows * cols + rows + cols + 1)
    return -(-used // 128) * 128


def flux_sweep(state, x_lo, x_hi, y_lo, y_hi):
    channels, rows, cols, depth = state.shape
    return pl.pallas_call(
        flux_kernel,
        out_shape=(
            jax.ShapeDtypeStruct(state.shape, state.dtype),
            jax.ShapeDtypeStruct((channels, cols, depth), state.dtype),
            jax.ShapeDtypeStruct((channels, rows, depth), state.dtype),
            jax.ShapeDtypeStruct((channels, depth), state.dtype),
            jax.ShapeDtypeStruct((table_rows(channels, rows, cols), depth), state.dtype),
        ),
    )(state, x_lo, x_hi, y_lo, y_hi)


def packed_permute(arrays, axis, by):
    flat = jnp.concatenate([array.reshape(-1) for array in arrays])
    moved = from_behind(flat, axis, by)
    parts, offset = [], 0
    for array in arrays:
        parts.append(moved[offset : offset + array.size].reshape(array.shape))
        offset += array.size
    return parts


def from_diagonal(array):
    count_x = lax.axis_size("gx")
    count_y = lax.axis_size("gy")
    pairs = [
        ((i + 1) * count_y + j + 1, i * count_y + j)
        for i in range(count_x - 1)
        for j in range(count_y - 1)
    ]
    return lax.ppermute(array, ("gx", "gy"), pairs)


def answer_requests(table, shape, arrived):
    channels, cells_x, cells_y, cells_z = shape
    count = arrived.shape[1]
    cell_index = arrived[3].astype(jnp.int32)
    base_x = cell_index // (cells_y * cells_z)
    base_y = cell_index // cells_z % cells_y
    base_z = cell_index % cells_z
    frac_x, frac_y, frac_z = arrived[0], arrived[1], arrived[2]
    z_ids = lax.broadcasted_iota(jnp.int32, (cells_z, count), 0)
    z_weight = jnp.where(z_ids == base_z[None, :], 1.0 - frac_z[None, :], 0.0) + jnp.where(
        z_ids == base_z[None, :] + 1, frac_z[None, :], 0.0
    )
    columns = lax.dot_general(
        table,
        z_weight,
        (((1,), (0,)), ((), ())),
        precision=lax.Precision.HIGH,
        preferred_element_type=jnp.float32,
    )
    x_ids = lax.broadcasted_iota(jnp.int32, (cells_x, count), 0)
    y_ids = lax.broadcasted_iota(jnp.int32, (cells_y, count), 0)
    weight_x = jnp.where(x_ids == base_x, 1.0 - frac_x, 0.0) + jnp.where(x_ids == base_x + 1, frac_x, 0.0)
    weight_y = jnp.where(y_ids == base_y, 1.0 - frac_y, 0.0) + jnp.where(y_ids == base_y + 1, frac_y, 0.0)
    edge_x = jnp.where(base_x + 1 == cells_x, frac_x, 0.0)
    edge_y = jnp.where(base_y + 1 == cells_y, frac_y, 0.0)
    weight_main = (weight_x[:, None, :] * weight_y[None, :, :]).reshape(cells_x * cells_y, count)
    weight_extra = jnp.concatenate(
        [edge_x[None] * weight_y, weight_x * edge_y[None], (edge_x * edge_y)[None]], axis=0
    )
    main_rows = cells_x * cells_y
    extra_rows = cells_x + cells_y + 1
    values = []
    for c in range(channels):
        main = columns[c * main_rows : (c + 1) * main_rows]
        start = channels * main_rows + c * extra_rows
        extra = columns[start : start + extra_rows]
        values.append(jnp.sum(main * weight_main, axis=0) + jnp.sum(extra * weight_extra, axis=0))
    return jnp.stack(values)


def pair_sums(own_tiles, other_tiles):
    separations = [own_tiles[c][:, None, :] - other_tiles[c][:, :, None] for c in range(3)]
    distance = jnp.sqrt(sum(separation * separation for separation in separations))
    closeness = jnp.maximum(1.0 - distance, 0.0)
    weight = 20.0 * closeness * closeness * closeness * other_tiles[7][:, :, None]
    push_term = (own_tiles[6][:, None, :] + other_tiles[6][:, :, None]) * weight
    weight_total = jnp.sum(weight, axis=1)
    result = []
    for channel, separation in enumerate(separations):
        drag_term = (
            jnp.sum(weight * other_tiles[3 + channel][:, :, None], axis=1)
            - weight_total * own_tiles[3 + channel]
        )
        result.append(jnp.sum(push_term * separation, axis=1) + VISCOSITY * drag_term)
    return jnp.stack(result)


def pieces(values):
    high = lax.reduce_precision(values, exponent_bits=8, mantissa_bits=7)
    rest = values - high
    middle = lax.reduce_precision(rest, exponent_bits=8, mantissa_bits=7)
    low = rest - middle
    return jnp.concatenate([high, middle, low], axis=0).astype(jnp.bfloat16)


def joined(parts, count):
    return (parts[:count] + parts[count : 2 * count]) + parts[2 * count :]


def step_body(
    fv_state,
    buffer_owner,
    buffer_cell,
    buffer_frac,
    buffer_count,
    sph_offset,
    sph_vel,
    sph_press,
    tile_count,
):
    grid_x = lax.axis_size("gx")
    grid_y = lax.axis_size("gy")
    tiles_x, tiles_y, tile_slots = sph_press.shape
    tile_live = (
        jnp.arange(tile_slots, dtype=jnp.int32)[None, None, :] < tile_count[:, :, None]
    ).astype(jnp.float32)
    packed = jnp.concatenate([sph_offset, sph_vel, sph_press[None], tile_live[None]], axis=0)
    devices = grid_x * grid_y
    buffer_rows = buffer_cell.shape[0]
    capacity = 2 * buffer_rows // devices
    slot_total = devices * capacity
    owner_ids = buffer_owner[:, 0]
    row_ids = jnp.arange(buffer_rows, dtype=jnp.int32)
    is_live = row_ids < buffer_count[0]
    one_hot = (owner_ids[:, None] == jnp.arange(devices, dtype=jnp.int32)[None, :]) & is_live[
        :, None
    ]
    one_hot_float = one_hot.astype(jnp.bfloat16)
    lower_mask = (row_ids[None, :] < row_ids[:, None]).astype(jnp.bfloat16)
    earlier = jnp.dot(lower_mask, one_hot_float, preferred_element_type=jnp.float32)
    ranks = jnp.sum(jnp.where(one_hot, earlier, 0.0), axis=1).astype(jnp.int32)
    target = jnp.where(is_live, owner_ids * capacity + ranks, slot_total)
    selector = (target[:, None] == jnp.arange(slot_total, dtype=jnp.int32)[None, :]).astype(
        jnp.bfloat16
    )
    request = jnp.concatenate([buffer_frac, buffer_cell[None].astype(jnp.float32)], axis=0)
    outgoing = joined(
        jnp.dot(pieces(request), selector, preferred_element_type=jnp.float32), request.shape[0]
    )
    arrived = lax.all_to_all(outgoing, ("gx", "gy"), split_axis=1, concat_axis=1, tiled=True)
    fv_state, packed, arrived = lax.optimization_barrier((fv_state, packed, arrived))
    x_lo, sph_before = packed_permute([fv_state[:, -1:], packed[:, -1:]], "gx", 1)
    x_hi, sph_after = packed_permute([fv_state[:, :1], packed[:, :1]], "gx", -1)
    framed = jnp.concatenate([sph_before, packed, sph_after], axis=1)
    y_lo, sph_left = packed_permute([fv_state[:, :, -1:], framed[:, :, -1:]], "gy", 1)
    y_hi, sph_right = packed_permute([fv_state[:, :, :1], framed[:, :, :1]], "gy", -1)
    framed = jnp.concatenate([sph_left, framed, sph_right], axis=2)
    fv_next, first_row, first_column, first_corner, table = flux_sweep(
        fv_state, x_lo, x_hi, y_lo, y_hi
    )
    row_next = from_behind(first_row, "gx", -1)
    column_next = from_behind(first_column, "gy", -1)
    corner_next = from_diagonal(first_corner)
    extra = jnp.concatenate([row_next, column_next, corner_next[:, None]], axis=1)
    table = lax.dynamic_update_slice(
        table, extra.reshape(-1, extra.shape[-1]), (fv_next.size // fv_next.shape[-1], 0)
    )
    returned = lax.all_to_all(
        answer_requests(table, fv_next.shape, arrived), ("gx", "gy"), split_axis=1, concat_axis=1, tiled=True
    )
    picked = joined(
        lax.dot_general(
            pieces(returned),
            selector,
            (((1,), (1,)), ((), ())),
            preferred_element_type=jnp.float32,
        ),
        returned.shape[0],
    )
    buffer_state = jnp.where(is_live[None, :], picked, 0.0)
    own_tiles = packed.reshape(8, tiles_x * tiles_y, tile_slots)
    neighbours = []
    for corner in range(9):
        step_x = corner // 3 - 1
        step_y = corner % 3 - 1
        window = framed[:, 1 + step_x : 1 + step_x + tiles_x, 1 + step_y : 1 + step_y + tiles_y]
        shift = jnp.array([step_x, step_y, 0, 0, 0, 0, 0, 0], jnp.float32)[:, None, None, None]
        neighbours.append(window + shift)
    other_tiles = jnp.stack(neighbours, axis=3).reshape(8, tiles_x * tiles_y, 9 * tile_slots)
    total = pair_sums(own_tiles, other_tiles)
    sph_accel = (FORCE_SCALE * total * own_tiles[7][None]).reshape(3, tiles_x, tiles_y, tile_slots)
    return (fv_next, buffer_state, sph_accel)


def solution(mesh):
    return sharded(mesh)


def sharded(mesh):
    return jax.shard_map(
        step_body,
        mesh=mesh,
        in_specs=(
            P(None, "gx", "gy", None),
            P(("gx", "gy"), None),
            P(("gx", "gy")),
            P(None, ("gx", "gy")),
            P(("gx", "gy")),
            P(None, "gx", "gy", None),
            P(None, "gx", "gy", None),
            P("gx", "gy", None),
            P("gx", "gy"),
        ),
        out_specs=(P(None, "gx", "gy", None), P(None, ("gx", "gy")), P(None, "gx", "gy", None)),
        check_vma=False,
    )
```

```python
import jax
import jax.numpy as jnp
from jax import lax
from jax.experimental import pallas as pl
from jax.experimental.pallas import tpu as pltpu
from jax.sharding import PartitionSpec as P


STEP_RATIO = 0.3
VISCOSITY = 0.02
FORCE_SCALE = 0.1


def from_behind(array, axis, by):
    count = lax.axis_size(axis)
    pairs = [(i, i + by) for i in range(count) if 0 <= i + by < count]
    return lax.ppermute(array, axis, pairs)


def flux_kernel(
    state_ref, x_lo_ref, x_hi_ref, y_lo_ref, y_hi_ref, out_ref, row_ref, column_ref, corner_ref, table_ref
):
    channels, rows, cols, depth = state_ref.shape
    main_rows = channels * rows * cols
    table_ref[main_rows:, :] = jnp.zeros((table_ref.shape[0] - main_rows, depth), jnp.float32)
    col_ids = lax.broadcasted_iota(jnp.int32, (cols, depth), 0)
    lane_ids = lax.broadcasted_iota(jnp.int32, (cols, depth), 1)
    for x in range(rows):
        centre = [state_ref[c, x] for c in range(channels)]
        ahead = [state_ref[c, x + 1] if x + 1 < rows else x_hi_ref[c, 0] for c in range(channels)]
        behind = [state_ref[c, x - 1] if x > 0 else x_lo_ref[c, 0] for c in range(channels)]
        up_y = [
            jnp.where(col_ids == cols - 1, y_hi_ref[c, x], pltpu.roll(centre[c], cols - 1, 0))
            for c in range(channels)
        ]
        down_y = [
            jnp.where(col_ids == 0, y_lo_ref[c, x], pltpu.roll(centre[c], 1, 0))
            for c in range(channels)
        ]
        up_z = [
            jnp.where(lane_ids == depth - 1, 0.0, pltpu.roll(centre[c], depth - 1, 1))
            for c in range(channels)
        ]
        down_z = [jnp.where(lane_ids == 0, 0.0, pltpu.roll(centre[c], 1, 1)) for c in range(channels)]
        change = None
        for normal, (lower, upper) in ((1, (behind, ahead)), (2, (down_y, up_y)), (3, (down_z, up_z))):
            high = face_flux_list(centre, upper, normal)
            low = face_flux_list(lower, centre, normal)
            step = [high[c] - low[c] for c in range(channels)]
            change = step if change is None else [change[c] + step[c] for c in range(channels)]
        for c in range(channels):
            result = centre[c] - STEP_RATIO * change[c]
            out_ref[c, x] = result
            table_ref[(c * rows + x) * cols : (c * rows + x + 1) * cols, :] = result
            column_ref[c, x : x + 1] = result[0:1]
            if x == 0:
                row_ref[c] = result
                corner_ref[c : c + 1] = result[0:1]


def face_flux_list(left_side, right_side, normal):
    fluxes = [-0.5 * (right_side[c] - left_side[c]) for c in range(len(left_side))]
    fluxes[0] = fluxes[0] + 0.5 * (left_side[normal] + right_side[normal])
    fluxes[normal] = fluxes[normal] + 0.5 * (left_side[0] + right_side[0])
    return fluxes


def table_rows(channels, rows, cols):
    used = channels * (rows * cols + rows + cols + 1)
    return -(-used // 128) * 128


def flux_sweep(state, x_lo, x_hi, y_lo, y_hi):
    channels, rows, cols, depth = state.shape
    return pl.pallas_call(
        flux_kernel,
        out_shape=(
            jax.ShapeDtypeStruct(state.shape, state.dtype),
            jax.ShapeDtypeStruct((channels, cols, depth), state.dtype),
            jax.ShapeDtypeStruct((channels, rows, depth), state.dtype),
            jax.ShapeDtypeStruct((channels, depth), state.dtype),
            jax.ShapeDtypeStruct((table_rows(channels, rows, cols), depth), state.dtype),
        ),
    )(state, x_lo, x_hi, y_lo, y_hi)


def exchange(values, devices):
    channels, slots = values.shape
    rows = values.reshape(channels, devices, slots // devices).transpose(1, 0, 2)
    moved = lax.all_to_all(rows.reshape(devices, -1), ("gx", "gy"), 0, 0, tiled=True)
    return moved.reshape(devices, channels, slots // devices).transpose(1, 0, 2).reshape(channels, slots)


def packed_permute(arrays, axis, by):
    flat = jnp.concatenate([array.reshape(-1) for array in arrays])
    moved = from_behind(flat, axis, by)
    parts, offset = [], 0
    for array in arrays:
        parts.append(moved[offset : offset + array.size].reshape(array.shape))
        offset += array.size
    return parts


def from_diagonal(array):
    count_x = lax.axis_size("gx")
    count_y = lax.axis_size("gy")
    pairs = [
        ((i + 1) * count_y + j + 1, i * count_y + j)
        for i in range(count_x - 1)
        for j in range(count_y - 1)
    ]
    return lax.ppermute(array, ("gx", "gy"), pairs)


def answer_requests(table, shape, arrived):
    channels, cells_x, cells_y, cells_z = shape
    count = arrived.shape[1]
    cell_index = arrived[3].astype(jnp.int32)
    base_x = cell_index // (cells_y * cells_z)
    base_y = cell_index // cells_z % cells_y
    base_z = cell_index % cells_z
    frac_x, frac_y, frac_z = arrived[0], arrived[1], arrived[2]
    z_ids = lax.broadcasted_iota(jnp.int32, (cells_z, count), 0)
    z_weight = jnp.where(z_ids == base_z[None, :], 1.0 - frac_z[None, :], 0.0) + jnp.where(
        z_ids == base_z[None, :] + 1, frac_z[None, :], 0.0
    )
    columns = lax.dot_general(
        table,
        z_weight,
        (((1,), (0,)), ((), ())),
        precision=lax.Precision.HIGH,
        preferred_element_type=jnp.float32,
    )
    x_ids = lax.broadcasted_iota(jnp.int32, (cells_x, count), 0)
    y_ids = lax.broadcasted_iota(jnp.int32, (cells_y, count), 0)
    weight_x = jnp.where(x_ids == base_x, 1.0 - frac_x, 0.0) + jnp.where(x_ids == base_x + 1, frac_x, 0.0)
    weight_y = jnp.where(y_ids == base_y, 1.0 - frac_y, 0.0) + jnp.where(y_ids == base_y + 1, frac_y, 0.0)
    edge_x = jnp.where(base_x + 1 == cells_x, frac_x, 0.0)
    edge_y = jnp.where(base_y + 1 == cells_y, frac_y, 0.0)
    weight_main = (weight_x[:, None, :] * weight_y[None, :, :]).reshape(cells_x * cells_y, count)
    weight_extra = jnp.concatenate(
        [edge_x[None] * weight_y, weight_x * edge_y[None], (edge_x * edge_y)[None]], axis=0
    )
    main_rows = cells_x * cells_y
    extra_rows = cells_x + cells_y + 1
    values = []
    for c in range(channels):
        main = columns[c * main_rows : (c + 1) * main_rows]
        start = channels * main_rows + c * extra_rows
        extra = columns[start : start + extra_rows]
        values.append(jnp.sum(main * weight_main, axis=0) + jnp.sum(extra * weight_extra, axis=0))
    return jnp.stack(values)


def pair_sums(own_tiles, other_tiles):
    separations = [own_tiles[c][:, None, :] - other_tiles[c][:, :, None] for c in range(3)]
    distance = jnp.sqrt(sum(separation * separation for separation in separations))
    closeness = jnp.maximum(1.0 - distance, 0.0)
    weight = 20.0 * closeness * closeness * closeness * other_tiles[7][:, :, None]
    push_term = (own_tiles[6][:, None, :] + other_tiles[6][:, :, None]) * weight
    weight_total = jnp.sum(weight, axis=1)
    result = []
    for channel, separation in enumerate(separations):
        drag_term = (
            jnp.sum(weight * other_tiles[3 + channel][:, :, None], axis=1)
            - weight_total * own_tiles[3 + channel]
        )
        result.append(jnp.sum(push_term * separation, axis=1) + VISCOSITY * drag_term)
    return jnp.stack(result)


def pieces(values):
    high = lax.reduce_precision(values, exponent_bits=8, mantissa_bits=7)
    rest = values - high
    middle = lax.reduce_precision(rest, exponent_bits=8, mantissa_bits=7)
    low = rest - middle
    return jnp.concatenate([high, middle, low], axis=0).astype(jnp.bfloat16)


def joined(parts, count):
    return (parts[:count] + parts[count : 2 * count]) + parts[2 * count :]


def step_body(
    fv_state,
    buffer_owner,
    buffer_cell,
    buffer_frac,
    buffer_count,
    sph_offset,
    sph_vel,
    sph_press,
    tile_count,
):
    grid_x = lax.axis_size("gx")
    grid_y = lax.axis_size("gy")
    tiles_x, tiles_y, tile_slots = sph_press.shape
    tile_live = (
        jnp.arange(tile_slots, dtype=jnp.int32)[None, None, :] < tile_count[:, :, None]
    ).astype(jnp.float32)
    packed = jnp.concatenate([sph_offset, sph_vel, sph_press[None], tile_live[None]], axis=0)
    x_lo, sph_before = packed_permute([fv_state[:, -1:], packed[:, -1:]], "gx", 1)
    x_hi, sph_after = packed_permute([fv_state[:, :1], packed[:, :1]], "gx", -1)
    framed = jnp.concatenate([sph_before, packed, sph_after], axis=1)
    y_lo, sph_left = packed_permute([fv_state[:, :, -1:], framed[:, :, -1:]], "gy", 1)
    y_hi, sph_right = packed_permute([fv_state[:, :, :1], framed[:, :, :1]], "gy", -1)
    framed = jnp.concatenate([sph_left, framed, sph_right], axis=2)
    devices = grid_x * grid_y
    buffer_rows = buffer_cell.shape[0]
    capacity = 2 * buffer_rows // devices
    slot_total = devices * capacity
    owner_ids = buffer_owner[:, 0]
    row_ids = jnp.arange(buffer_rows, dtype=jnp.int32)
    is_live = row_ids < buffer_count[0]
    one_hot = (owner_ids[:, None] == jnp.arange(devices, dtype=jnp.int32)[None, :]) & is_live[
        :, None
    ]
    one_hot_float = one_hot.astype(jnp.bfloat16)
    lower_mask = (row_ids[None, :] < row_ids[:, None]).astype(jnp.bfloat16)
    earlier = jnp.dot(lower_mask, one_hot_float, preferred_element_type=jnp.float32)
    ranks = jnp.sum(jnp.where(one_hot, earlier, 0.0), axis=1).astype(jnp.int32)
    target = jnp.where(is_live, owner_ids * capacity + ranks, slot_total)
    selector = (target[:, None] == jnp.arange(slot_total, dtype=jnp.int32)[None, :]).astype(
        jnp.bfloat16
    )
    request = jnp.concatenate([buffer_frac, buffer_cell[None].astype(jnp.float32)], axis=0)
    outgoing = joined(
        jnp.dot(pieces(request), selector, preferred_element_type=jnp.float32), request.shape[0]
    )
    arrived = exchange(outgoing, devices)
    fv_next, first_row, first_column, first_corner, table = flux_sweep(
        fv_state, x_lo, x_hi, y_lo, y_hi
    )
    row_next = from_behind(first_row, "gx", -1)
    column_next = from_behind(first_column, "gy", -1)
    corner_next = from_diagonal(first_corner)
    extra = jnp.concatenate([row_next, column_next, corner_next[:, None]], axis=1)
    table = lax.dynamic_update_slice(
        table, extra.reshape(-1, extra.shape[-1]), (fv_next.size // fv_next.shape[-1], 0)
    )
    returned = exchange(answer_requests(table, fv_next.shape, arrived), devices)
    picked = joined(
        lax.dot_general(
            pieces(returned),
            selector,
            (((1,), (1,)), ((), ())),
            preferred_element_type=jnp.float32,
        ),
        returned.shape[0],
    )
    buffer_state = jnp.where(is_live[None, :], picked, 0.0)
    own_tiles = packed.reshape(8, tiles_x * tiles_y, tile_slots)
    neighbours = []
    for corner in range(9):
        step_x = corner // 3 - 1
        step_y = corner % 3 - 1
        window = framed[:, 1 + step_x : 1 + step_x + tiles_x, 1 + step_y : 1 + step_y + tiles_y]
        shift = jnp.array([step_x, step_y, 0, 0, 0, 0, 0, 0], jnp.float32)[:, None, None, None]
        neighbours.append(window + shift)
    other_tiles = jnp.stack(neighbours, axis=3).reshape(8, tiles_x * tiles_y, 9 * tile_slots)
    total = pair_sums(own_tiles, other_tiles)
    sph_accel = (FORCE_SCALE * total * own_tiles[7][None]).reshape(3, tiles_x, tiles_y, tile_slots)
    return (fv_next, buffer_state, sph_accel)


def solution(mesh):
    return sharded(mesh)


def sharded(mesh):
    return jax.shard_map(
        step_body,
        mesh=mesh,
        in_specs=(
            P(None, "gx", "gy", None),
            P(("gx", "gy"), None),
            P(("gx", "gy")),
            P(None, ("gx", "gy")),
            P(("gx", "gy")),
            P(None, "gx", "gy", None),
            P(None, "gx", "gy", None),
            P("gx", "gy", None),
            P("gx", "gy"),
        ),
        out_specs=(P(None, "gx", "gy", None), P(None, ("gx", "gy")), P(None, "gx", "gy", None)),
        check_vma=False,
    )
```

```python
import jax
import jax.numpy as jnp
from jax import lax
from jax.experimental import pallas as pl
from jax.experimental.pallas import tpu as pltpu
from jax.sharding import PartitionSpec as P


STEP_RATIO = 0.3
VISCOSITY = 0.02
FORCE_SCALE = 0.1


def from_behind(array, axis, by):
    count = lax.axis_size(axis)
    pairs = [(i, i + by) for i in range(count) if 0 <= i + by < count]
    return lax.ppermute(array, axis, pairs)


def flux_kernel(
    state_ref, x_lo_ref, x_hi_ref, y_lo_ref, y_hi_ref, out_ref, row_ref, column_ref, corner_ref, table_ref
):
    channels, rows, cols, depth = state_ref.shape
    main_rows = channels * rows * cols
    table_ref[main_rows:, :] = jnp.zeros((table_ref.shape[0] - main_rows, depth), jnp.float32)
    col_ids = lax.broadcasted_iota(jnp.int32, (cols, depth), 0)
    lane_ids = lax.broadcasted_iota(jnp.int32, (cols, depth), 1)
    for x in range(rows):
        centre = [state_ref[c, x] for c in range(channels)]
        ahead = [state_ref[c, x + 1] if x + 1 < rows else x_hi_ref[c, 0] for c in range(channels)]
        behind = [state_ref[c, x - 1] if x > 0 else x_lo_ref[c, 0] for c in range(channels)]
        up_y = [
            jnp.where(col_ids == cols - 1, y_hi_ref[c, x], pltpu.roll(centre[c], cols - 1, 0))
            for c in range(channels)
        ]
        down_y = [
            jnp.where(col_ids == 0, y_lo_ref[c, x], pltpu.roll(centre[c], 1, 0))
            for c in range(channels)
        ]
        up_z = [
            jnp.where(lane_ids == depth - 1, 0.0, pltpu.roll(centre[c], depth - 1, 1))
            for c in range(channels)
        ]
        down_z = [jnp.where(lane_ids == 0, 0.0, pltpu.roll(centre[c], 1, 1)) for c in range(channels)]
        change = None
        for normal, (lower, upper) in ((1, (behind, ahead)), (2, (down_y, up_y)), (3, (down_z, up_z))):
            high = face_flux_list(centre, upper, normal)
            low = face_flux_list(lower, centre, normal)
            step = [high[c] - low[c] for c in range(channels)]
            change = step if change is None else [change[c] + step[c] for c in range(channels)]
        for c in range(channels):
            result = centre[c] - STEP_RATIO * change[c]
            out_ref[c, x] = result
            table_ref[(c * rows + x) * cols : (c * rows + x + 1) * cols, :] = result
            column_ref[c, x : x + 1] = result[0:1]
            if x == 0:
                row_ref[c] = result
                corner_ref[c : c + 1] = result[0:1]


def face_flux_list(left_side, right_side, normal):
    fluxes = [-0.5 * (right_side[c] - left_side[c]) for c in range(len(left_side))]
    fluxes[0] = fluxes[0] + 0.5 * (left_side[normal] + right_side[normal])
    fluxes[normal] = fluxes[normal] + 0.5 * (left_side[0] + right_side[0])
    return fluxes


def table_rows(channels, rows, cols):
    used = channels * (rows * cols + rows + cols + 1)
    return -(-used // 128) * 128


def flux_sweep(state, x_lo, x_hi, y_lo, y_hi):
    channels, rows, cols, depth = state.shape
    return pl.pallas_call(
        flux_kernel,
        out_shape=(
            jax.ShapeDtypeStruct(state.shape, state.dtype),
            jax.ShapeDtypeStruct((channels, cols, depth), state.dtype),
            jax.ShapeDtypeStruct((channels, rows, depth), state.dtype),
            jax.ShapeDtypeStruct((channels, depth), state.dtype),
            jax.ShapeDtypeStruct((table_rows(channels, rows, cols), depth), state.dtype),
        ),
    )(state, x_lo, x_hi, y_lo, y_hi)


def exchange(values, devices):
    channels, slots = values.shape
    rows = values.reshape(channels, devices, slots // devices).transpose(1, 0, 2)
    moved = lax.all_to_all(rows.reshape(devices, -1), ("gx", "gy"), 0, 0, tiled=True)
    return moved.reshape(devices, channels, slots // devices).transpose(1, 0, 2).reshape(channels, slots)


def packed_permute(arrays, axis, by):
    width = arrays[0].shape[-1]
    flat = jnp.concatenate([array.reshape(-1, width) for array in arrays], axis=0)
    moved = from_behind(flat, axis, by)
    parts, offset = [], 0
    for array in arrays:
        rows = array.size // width
        parts.append(moved[offset : offset + rows].reshape(array.shape))
        offset += rows
    return parts


def from_diagonal(array):
    count_x = lax.axis_size("gx")
    count_y = lax.axis_size("gy")
    pairs = [
        ((i + 1) * count_y + j + 1, i * count_y + j)
        for i in range(count_x - 1)
        for j in range(count_y - 1)
    ]
    return lax.ppermute(array, ("gx", "gy"), pairs)


def answer_requests(table, shape, arrived):
    channels, cells_x, cells_y, cells_z = shape
    count = arrived.shape[1]
    cell_index = arrived[3].astype(jnp.int32)
    base_x = cell_index // (cells_y * cells_z)
    base_y = cell_index // cells_z % cells_y
    base_z = cell_index % cells_z
    frac_x, frac_y, frac_z = arrived[0], arrived[1], arrived[2]
    z_ids = lax.broadcasted_iota(jnp.int32, (cells_z, count), 0)
    z_weight = jnp.where(z_ids == base_z[None, :], 1.0 - frac_z[None, :], 0.0) + jnp.where(
        z_ids == base_z[None, :] + 1, frac_z[None, :], 0.0
    )
    columns = lax.dot_general(
        table,
        z_weight,
        (((1,), (0,)), ((), ())),
        precision=lax.Precision.HIGH,
        preferred_element_type=jnp.float32,
    )
    x_ids = lax.broadcasted_iota(jnp.int32, (cells_x, count), 0)
    y_ids = lax.broadcasted_iota(jnp.int32, (cells_y, count), 0)
    weight_x = jnp.where(x_ids == base_x, 1.0 - frac_x, 0.0) + jnp.where(x_ids == base_x + 1, frac_x, 0.0)
    weight_y = jnp.where(y_ids == base_y, 1.0 - frac_y, 0.0) + jnp.where(y_ids == base_y + 1, frac_y, 0.0)
    edge_x = jnp.where(base_x + 1 == cells_x, frac_x, 0.0)
    edge_y = jnp.where(base_y + 1 == cells_y, frac_y, 0.0)
    weight_main = (weight_x[:, None, :] * weight_y[None, :, :]).reshape(cells_x * cells_y, count)
    weight_extra = jnp.concatenate(
        [edge_x[None] * weight_y, weight_x * edge_y[None], (edge_x * edge_y)[None]], axis=0
    )
    main_rows = cells_x * cells_y
    extra_rows = cells_x + cells_y + 1
    values = []
    for c in range(channels):
        main = columns[c * main_rows : (c + 1) * main_rows]
        start = channels * main_rows + c * extra_rows
        extra = columns[start : start + extra_rows]
        values.append(jnp.sum(main * weight_main, axis=0) + jnp.sum(extra * weight_extra, axis=0))
    return jnp.stack(values)


def pair_sums(own_tiles, other_tiles):
    separations = [own_tiles[c][:, None, :] - other_tiles[c][:, :, None] for c in range(3)]
    distance = jnp.sqrt(sum(separation * separation for separation in separations))
    closeness = jnp.maximum(1.0 - distance, 0.0)
    weight = 20.0 * closeness * closeness * closeness * other_tiles[7][:, :, None]
    push_term = (own_tiles[6][:, None, :] + other_tiles[6][:, :, None]) * weight
    weight_total = jnp.sum(weight, axis=1)
    result = []
    for channel, separation in enumerate(separations):
        drag_term = (
            jnp.sum(weight * other_tiles[3 + channel][:, :, None], axis=1)
            - weight_total * own_tiles[3 + channel]
        )
        result.append(jnp.sum(push_term * separation, axis=1) + VISCOSITY * drag_term)
    return jnp.stack(result)


def pieces(values):
    high = lax.reduce_precision(values, exponent_bits=8, mantissa_bits=7)
    rest = values - high
    middle = lax.reduce_precision(rest, exponent_bits=8, mantissa_bits=7)
    low = rest - middle
    return jnp.concatenate([high, middle, low], axis=0).astype(jnp.bfloat16)


def joined(parts, count):
    return (parts[:count] + parts[count : 2 * count]) + parts[2 * count :]


def step_body(
    fv_state,
    buffer_owner,
    buffer_cell,
    buffer_frac,
    buffer_count,
    sph_offset,
    sph_vel,
    sph_press,
    tile_count,
):
    grid_x = lax.axis_size("gx")
    grid_y = lax.axis_size("gy")
    tiles_x, tiles_y, tile_slots = sph_press.shape
    tile_live = (
        jnp.arange(tile_slots, dtype=jnp.int32)[None, None, :] < tile_count[:, :, None]
    ).astype(jnp.float32)
    packed = jnp.concatenate([sph_offset, sph_vel, sph_press[None], tile_live[None]], axis=0)
    x_lo, sph_before = packed_permute([fv_state[:, -1:], packed[:, -1:]], "gx", 1)
    x_hi, sph_after = packed_permute([fv_state[:, :1], packed[:, :1]], "gx", -1)
    framed = jnp.concatenate([sph_before, packed, sph_after], axis=1)
    y_lo, sph_left = packed_permute([fv_state[:, :, -1:], framed[:, :, -1:]], "gy", 1)
    y_hi, sph_right = packed_permute([fv_state[:, :, :1], framed[:, :, :1]], "gy", -1)
    framed = jnp.concatenate([sph_left, framed, sph_right], axis=2)
    devices = grid_x * grid_y
    buffer_rows = buffer_cell.shape[0]
    capacity = 2 * buffer_rows // devices
    slot_total = devices * capacity
    owner_ids = buffer_owner[:, 0]
    row_ids = jnp.arange(buffer_rows, dtype=jnp.int32)
    is_live = row_ids < buffer_count[0]
    one_hot = (owner_ids[:, None] == jnp.arange(devices, dtype=jnp.int32)[None, :]) & is_live[
        :, None
    ]
    one_hot_float = one_hot.astype(jnp.bfloat16)
    lower_mask = (row_ids[None, :] < row_ids[:, None]).astype(jnp.bfloat16)
    earlier = jnp.dot(lower_mask, one_hot_float, preferred_element_type=jnp.float32)
    ranks = jnp.sum(jnp.where(one_hot, earlier, 0.0), axis=1).astype(jnp.int32)
    target = jnp.where(is_live, owner_ids * capacity + ranks, slot_total)
    selector = (target[:, None] == jnp.arange(slot_total, dtype=jnp.int32)[None, :]).astype(
        jnp.bfloat16
    )
    request = jnp.concatenate([buffer_frac, buffer_cell[None].astype(jnp.float32)], axis=0)
    outgoing = joined(
        jnp.dot(pieces(request), selector, preferred_element_type=jnp.float32), request.shape[0]
    )
    arrived = exchange(outgoing, devices)
    fv_next, first_row, first_column, first_corner, table = flux_sweep(
        fv_state, x_lo, x_hi, y_lo, y_hi
    )
    row_next = from_behind(first_row, "gx", -1)
    column_next = from_behind(first_column, "gy", -1)
    corner_next = from_diagonal(first_corner)
    extra = jnp.concatenate([row_next, column_next, corner_next[:, None]], axis=1)
    table = lax.dynamic_update_slice(
        table, extra.reshape(-1, extra.shape[-1]), (fv_next.size // fv_next.shape[-1], 0)
    )
    returned = exchange(answer_requests(table, fv_next.shape, arrived), devices)
    picked = joined(
        lax.dot_general(
            pieces(returned),
            selector,
            (((1,), (1,)), ((), ())),
            preferred_element_type=jnp.float32,
        ),
        returned.shape[0],
    )
    buffer_state = jnp.where(is_live[None, :], picked, 0.0)
    own_tiles = packed.reshape(8, tiles_x * tiles_y, tile_slots)
    neighbours = []
    for corner in range(9):
        step_x = corner // 3 - 1
        step_y = corner % 3 - 1
        window = framed[:, 1 + step_x : 1 + step_x + tiles_x, 1 + step_y : 1 + step_y + tiles_y]
        shift = jnp.array([step_x, step_y, 0, 0, 0, 0, 0, 0], jnp.float32)[:, None, None, None]
        neighbours.append(window + shift)
    other_tiles = jnp.stack(neighbours, axis=3).reshape(8, tiles_x * tiles_y, 9 * tile_slots)
    total = pair_sums(own_tiles, other_tiles)
    sph_accel = (FORCE_SCALE * total * own_tiles[7][None]).reshape(3, tiles_x, tiles_y, tile_slots)
    return (fv_next, buffer_state, sph_accel)


def solution(mesh):
    return sharded(mesh)


def sharded(mesh):
    return jax.shard_map(
        step_body,
        mesh=mesh,
        in_specs=(
            P(None, "gx", "gy", None),
            P(("gx", "gy"), None),
            P(("gx", "gy")),
            P(None, ("gx", "gy")),
            P(("gx", "gy")),
            P(None, "gx", "gy", None),
            P(None, "gx", "gy", None),
            P("gx", "gy", None),
            P("gx", "gy"),
        ),
        out_specs=(P(None, "gx", "gy", None), P(None, ("gx", "gy")), P(None, "gx", "gy", None)),
        check_vma=False,
    )
```
